32 devices in a mesh: groups: 2 (over y), ctx: 4 (over z), head: 4 (over x, core).
Axes of the slice: x: 2, y: 2, z: 4, core: 2. Of those that a mesh axis runs over, the one named last changes fastest.
Arguments:
- hidden_in: bfloat16 [4096, 4096], P(('groups', 'ctx'), 'head'), parts along dimension 0, may hold values from -6 to 6
- attn_gain: float32 [4096], replicated, may hold values from 0.5 to 12, as said below
- w_query: bfloat16 [4096, 2048], P(None, 'head'), may hold values from -0.09375 to 0.09375
- w_keys: bfloat16 [4096, 1024], P(None, 'head'), may hold values from -0.09375 to 0.09375
- w_values: bfloat16 [4096, 1024], P(None, 'head'), may hold values from -0.09375 to 0.09375
- wo_attn: bfloat16 [2048, 4096], P('head'), may hold values from -0.125 to 0.125
- lin_gain: float32 [4096], replicated, may hold values from 0.5 to 1.5
- w_feature: bfloat16 [4096, 256], P(None, 'head'), may hold values from -0.09375 to 0.09375
- wv_linear: bfloat16 [4096, 2048], P(None, 'head'), may hold values from -0.09375 to 0.09375
- out_gain: float32 [8, 256], P('head'), may hold values from 0.5 to 1.5
- wo_linear: bfloat16 [2048, 4096], P('head'), may hold values from -0.125 to 0.125
- entry_state: float32 [16, 273, 256], P(('groups', 'head')), parts along dimension 0, may hold values from -180 to 180
Outputs:
- mixed: bfloat16 [4096, 4096], P(('groups', 'ctx'), 'head'), parts along dimension 0
The draws below stay inside these ranges and needn't reach their ends.
There are 2 independent parts, one for each index of `groups`. The reference program is written for one: setup_inputs(seed, part) draws one part's arguments, and reference() takes and returns one part's arrays. A program takes and returns all parts, laid end to end along the dimension named above; an argument that names none is the same for every part. Nothing has to cross between parts.
Inputs may be any that keep to these rules, and one draw needn't show every extreme that they name: `attn_gain`: a positive gain for every feature.
All inputs are finite; a program needn't handle non-finite values.
Results may differ from the reference program's by a relative error of at most 0.008.
The reference program's roundings to bfloat16 on the way count: a program that leaves them out, or rounds other values in their place, can miss the bound.
Values may be sent and summed in bfloat16 or wider, within the bound.
No kernel may reach another device: no remote copies, remote signals or barrier semaphores. Data moves between devices by JAX's collectives and lax.ppermute only.
A program may use at most 128 MiB of HBM per device.

```python
import math
import jax
import jax.numpy as jnp
from jax import lax

D = 4096
WHEADS = 16
KVHEADS = 8
HEAD = 128
WINDOW = 64
LHEADS = 8
FEAT = 16
VDIM = 256
TOK_DEV = 512
FD = 273
TOKENS = 2048


def draw_attn_gain(key, part):
    return jax.random.uniform(key, (D,), jnp.float32, 0.5, 1.5)


def level_of(rng, dims, shards, low, top_value):
    level, own = 1.0, jax.random.fold_in(rng, 6)
    for dim, shards_of in shards:
        heights = jnp.exp(jax.random.uniform(jax.random.fold_in(own, dim), (shards_of,), jnp.float32, low / len(shards), top_value / len(shards)))
        level = level * jnp.repeat(heights, dims[dim] // shards_of).reshape([-1 if axis == dim else 1 for axis in range(len(dims))])
    return level


def bell_draw(key, dims, scale, reach, cuts=(), kind=jnp.bfloat16):
    factor_of = level_of(key, dims, cuts, -0.22, 0.18) if cuts else 1.0
    drawn = jax.random.normal(key, dims, jnp.float32) * scale * factor_of
    return jnp.minimum(jnp.maximum(drawn, -reach), reach).astype(kind)


def setup_inputs(seed: int = 0, part: int = 0) -> dict:
    arg_keys = jax.random.split(jax.random.key(seed), 13)
    part_keys = jax.random.split(jax.random.fold_in(arg_keys[12], part), 13)
    return {
        "hidden_in": bell_draw(part_keys[0], (TOKENS, D), 1.0, 6.0, ((0, 4), (1, 4))),
        "attn_gain": draw_attn_gain(jax.random.fold_in(arg_keys[12], 71), part),
        "w_query": bell_draw(arg_keys[2], (D, WHEADS * HEAD), D ** -0.5, 0.09375, ((1, 4),)),
        "w_keys": bell_draw(arg_keys[3], (D, KVHEADS * HEAD), D ** -0.5, 0.09375, ((1, 4),)),
        "w_values": bell_draw(arg_keys[4], (D, KVHEADS * HEAD), D ** -0.5, 0.09375, ((1, 4),)),
        "wo_attn": bell_draw(arg_keys[5], (WHEADS * HEAD, D), (WHEADS * HEAD) ** -0.5, 0.125, ((0, 4),)),
        "lin_gain": jnp.clip(jax.random.uniform(arg_keys[6], (D,), jnp.float32, 0.5, 1.5), 0.5, 1.5),
        "w_feature": bell_draw(arg_keys[7], (D, LHEADS * 2 * FEAT), D ** -0.5, 0.09375, ((1, 4),)),
        "wv_linear": bell_draw(arg_keys[8], (D, LHEADS * VDIM), D ** -0.5, 0.09375, ((1, 4),)),
        "out_gain": jnp.clip(0.5 + 1.0 * jax.random.uniform(arg_keys[9], (LHEADS, VDIM), jnp.float32) ** level_of(arg_keys[9], (LHEADS, VDIM), ((0, 4),), -0.2, 0.2), 0.5, 1.5),
        "wo_linear": bell_draw(arg_keys[10], (LHEADS * VDIM, D), (LHEADS * VDIM) ** -0.5, 0.125, ((0, 4),)),
        "entry_state": bell_draw(part_keys[11], (LHEADS, FD, VDIM), 30.0, 180.0, ((0, 4),), jnp.float32),
    }


def norm_rows(values, gain):
    wide = values.astype(jnp.float32)
    scale = lax.rsqrt(lax.optimization_barrier(jnp.mean(wide * wide, axis=-1, keepdims=True)) + 1e-05)
    return (wide * scale * gain.astype(jnp.float32)).astype(jnp.bfloat16)

def taylor(inputs):
    width = inputs.shape[-1]
    outer = (inputs[..., :, None] * inputs[..., None, :]).reshape(inputs.shape[:-1] + (width * width,))
    ones = jnp.ones(inputs.shape[:-1] + (1,), jnp.float32)
    return jnp.concatenate([ones, inputs / width ** 0.25, outer / (math.sqrt(2.0) * math.sqrt(width))], axis=-1)

def reference(hidden_in, attn_gain, w_query, w_keys, w_values, wo_attn, lin_gain, w_feature, wv_linear, out_gain, wo_linear, entry_state):
    normed = norm_rows(hidden_in, attn_gain)
    query = jnp.dot(normed, w_query, preferred_element_type=jnp.float32).astype(jnp.bfloat16)
    keys = jnp.dot(normed, w_keys, preferred_element_type=jnp.float32).astype(jnp.bfloat16)
    values = jnp.dot(normed, w_values, preferred_element_type=jnp.float32).astype(jnp.bfloat16)
    group = WHEADS // KVHEADS
    keys_pad = jnp.concatenate([jnp.zeros((WINDOW, KVHEADS * HEAD), jnp.bfloat16), keys], axis=0)
    values_pad = jnp.concatenate([jnp.zeros((WINDOW, KVHEADS * HEAD), jnp.bfloat16), values], axis=0)
    nblocks = TOKENS // TOK_DEV

    def window_block(block):
        start = (block * TOK_DEV).astype(jnp.int32)
        qpart = lax.dynamic_slice_in_dim(query, start, TOK_DEV, 0).reshape(TOK_DEV, KVHEADS, group, HEAD)
        kpart = lax.dynamic_slice_in_dim(keys_pad, start, TOK_DEV + WINDOW, 0).reshape(TOK_DEV + WINDOW, KVHEADS, HEAD)
        vpart = lax.dynamic_slice_in_dim(values_pad, start, TOK_DEV + WINDOW, 0).reshape(TOK_DEV + WINDOW, KVHEADS, HEAD)
        scores = jnp.einsum('tkgd,skd->kgts', qpart.astype(jnp.float32), kpart.astype(jnp.float32)) / math.sqrt(HEAD)
        qpos = start + jnp.arange(TOK_DEV, dtype=jnp.int32)
        kpos = start - WINDOW + jnp.arange(TOK_DEV + WINDOW, dtype=jnp.int32)
        visible = (kpos[None, :] <= qpos[:, None]) & (kpos[None, :] > qpos[:, None] - WINDOW) & (kpos[None, :] >= 0)
        scores = jnp.where(visible, scores, -jnp.inf)
        top = lax.optimization_barrier(jnp.max(scores, axis=-1, keepdims=True))
        expd = jnp.exp(scores - top)
        probs = (expd / lax.optimization_barrier(jnp.sum(expd, axis=-1, keepdims=True))).astype(jnp.bfloat16)
        out = jnp.einsum('kgts,skd->tkgd', probs.astype(jnp.float32), vpart.astype(jnp.float32))
        return out.astype(jnp.bfloat16).reshape(TOK_DEV, WHEADS * HEAD)
    attended = lax.map(window_block, jnp.arange(nblocks, dtype=jnp.int32)).reshape(TOKENS, WHEADS * HEAD)
    after_window = (hidden_in.astype(jnp.float32) + jnp.dot(attended, wo_attn, preferred_element_type=jnp.float32)).astype(jnp.bfloat16)
    normed2 = norm_rows(after_window, lin_gain)
    feats = jnp.dot(normed2, w_feature, preferred_element_type=jnp.float32).reshape(nblocks, TOK_DEV, LHEADS, 2, FEAT)
    lvalues = jnp.dot(normed2, wv_linear, preferred_element_type=jnp.float32).astype(jnp.bfloat16).reshape(nblocks, TOK_DEV, LHEADS, VDIM)
    causal = jnp.arange(TOK_DEV)[:, None] >= jnp.arange(TOK_DEV)[None, :]
    hp = lax.Precision.HIGHEST

    def linear_block(carried, inputs):
        part_feats, part_values = inputs
        qf = part_feats[:, :, 0, :]
        kf = part_feats[:, :, 1, :]
        phiq = taylor(qf)
        phik = taylor(kf)
        cross = jnp.einsum('thf,hfv->thv', phiq, carried, precision=hp)
        sims = jnp.einsum('thf,shf->hts', qf, kf, precision=hp) / math.sqrt(FEAT)
        weights = jnp.where(causal[None], 1.0 + sims + 0.5 * sims * sims, 0.0).astype(jnp.bfloat16)
        intra = jnp.einsum('hts,shv->thv', weights.astype(jnp.float32), part_values.astype(jnp.float32))
        lin_out = cross + intra
        scale = lax.rsqrt(lax.optimization_barrier(jnp.mean(lin_out * lin_out, axis=-1, keepdims=True)) + 1e-05)
        lin_normed = (lin_out * scale * out_gain[None]).astype(jnp.bfloat16).reshape(TOK_DEV, LHEADS * VDIM)
        local = jnp.einsum('thf,thv->hfv', phik, part_values.astype(jnp.float32), precision=hp)
        return (carried + local, lin_normed)
    final_state, lin_normed = lax.scan(linear_block, entry_state.astype(jnp.float32), (feats, lvalues))
    lin_normed = lin_normed.reshape(TOKENS, LHEADS * VDIM)
    return (after_window.astype(jnp.float32) + jnp.dot(lin_normed, wo_linear, preferred_element_type=jnp.float32)).astype(jnp.bfloat16)
```

```python
import math

import jax
import jax.numpy as jnp
from jax import lax
from jax.sharding import PartitionSpec as P

HEAD = 128
WINDOW = 64
FEAT = 16
VDIM = 256


def from_behind(value, axis, by):
    devices = lax.axis_size(axis)
    pairs = [(i, i + by) for i in range(devices) if 0 <= i + by < devices]
    return lax.ppermute(value, axis, pairs)


def head_layout():
    devices = lax.axis_size("head")
    return devices, devices // 2


def core_swap(value):
    devices = lax.axis_size("head")
    return lax.ppermute(value, "head", [(h, h ^ 1) for h in range(devices)])


def chip_shift(value, by):
    devices, chips = head_layout()
    pairs = [(h, ((h // 2 + by) % chips) * 2 + h % 2) for h in range(devices)]
    return lax.ppermute(value, "head", pairs)


def head_reduce_scatter(terms):
    rows, cols = terms.shape
    devices, chips = head_layout()
    me = lax.axis_index("head")
    core, chip = me % 2, me // 2
    split = terms.reshape(rows, chips, 2, cols // devices)
    mine = lax.dynamic_index_in_dim(split, core, axis=2, keepdims=False)
    other = lax.dynamic_index_in_dim(split, 1 - core, axis=2, keepdims=False)
    on_chip = mine + core_swap(other)
    if chips == 1:
        return on_chip[:, 0]
    acc = lax.dynamic_index_in_dim(on_chip, (chip + chips - 1) % chips, axis=1, keepdims=False)
    for step in range(chips - 1):
        got = chip_shift(acc, 1)
        index = (chip + 2 * chips - step - 2) % chips
        acc = got + lax.dynamic_index_in_dim(on_chip, index, axis=1, keepdims=False)
    return acc


def head_all_gather(piece):
    rows, cols = piece.shape
    devices, chips = head_layout()
    me = lax.axis_index("head")
    core, chip = me % 2, me // 2
    chip_buf = jnp.zeros((rows, chips, cols), piece.dtype)
    chip_buf = lax.dynamic_update_index_in_dim(chip_buf, piece, chip, axis=1)
    cur = piece
    for step in range(chips - 1):
        cur = chip_shift(cur, 1)
        chip_buf = lax.dynamic_update_index_in_dim(
            chip_buf, cur, (chip + 2 * chips - step - 1) % chips, axis=1
        )
    partner = core_swap(chip_buf)
    whole = jnp.zeros((rows, chips, 2, cols), piece.dtype)
    whole = lax.dynamic_update_index_in_dim(whole, chip_buf, core, axis=2)
    whole = lax.dynamic_update_index_in_dim(whole, partner, 1 - core, axis=2)
    return whole.reshape(rows, devices * cols)


def earlier_sum(local):
    count = lax.axis_size("ctx")
    sent = local.astype(jnp.bfloat16)
    total = jnp.zeros(local.shape, jnp.float32)
    for by in range(1, count):
        pairs = [(i, i + by) for i in range(count - by)]
        total = total + lax.ppermute(sent, "ctx", pairs).astype(jnp.float32)
    return total


def norm_rows(values, gain):
    wide = values.astype(jnp.float32)
    scale = lax.rsqrt(jnp.mean(wide * wide, axis=-1, keepdims=True) + 1e-05)
    return (wide * scale * gain).astype(jnp.bfloat16)


def taylor(inputs):
    width = inputs.shape[-1]
    outer = (inputs[..., :, None] * inputs[..., None, :]).reshape(
        inputs.shape[:-1] + (width * width,)
    )
    ones = jnp.ones(inputs.shape[:-1] + (1,), jnp.float32)
    return jnp.concatenate(
        [ones, inputs / width**0.25, outer / (math.sqrt(2.0) * math.sqrt(width))], axis=-1
    )


def body(
    hidden_in,
    attn_gain,
    w_query,
    w_keys,
    w_values,
    wo_attn,
    lin_gain,
    w_feature,
    wv_linear,
    out_gain,
    wo_linear,
    entry_state,
):
    tok_rows = hidden_in.shape[0]
    whole = head_all_gather(hidden_in)
    normed = norm_rows(whole, attn_gain)
    query = jnp.dot(normed, w_query, preferred_element_type=jnp.float32).astype(jnp.bfloat16)
    keys = jnp.dot(normed, w_keys, preferred_element_type=jnp.float32).astype(jnp.bfloat16)
    values = jnp.dot(normed, w_values, preferred_element_type=jnp.float32).astype(jnp.bfloat16)
    kv_cols = keys.shape[1]
    kv_heads = kv_cols // HEAD
    group = query.shape[1] // HEAD // kv_heads
    kv_pair = jnp.concatenate([keys, values], axis=1)
    rim = from_behind(kv_pair[tok_rows - WINDOW :], "ctx", 1)
    kv_all = jnp.concatenate([rim, kv_pair], axis=0)
    key_all = kv_all[:, :kv_cols].reshape(tok_rows + WINDOW, kv_heads, HEAD)
    value_all = kv_all[:, kv_cols:].reshape(tok_rows + WINDOW, kv_heads, HEAD)
    query_heads = query.reshape(tok_rows, kv_heads, group, HEAD)
    scores = jnp.einsum(
        "tkgd,skd->kgts", query_heads, key_all, preferred_element_type=jnp.float32
    ) / math.sqrt(HEAD)
    start = lax.axis_index("ctx") * tok_rows
    qpos = start + jnp.arange(tok_rows, dtype=jnp.int32)
    kpos = start - WINDOW + jnp.arange(tok_rows + WINDOW, dtype=jnp.int32)
    visible = (
        (kpos[None, :] <= qpos[:, None])
        & (kpos[None, :] > qpos[:, None] - WINDOW)
        & (kpos[None, :] >= 0)
    )
    scores = jnp.where(visible, scores, -jnp.inf)
    top = jnp.max(scores, axis=-1, keepdims=True)
    expd = jnp.exp(scores - top)
    probs = (expd / jnp.sum(expd, axis=-1, keepdims=True)).astype(jnp.bfloat16)
    attended = jnp.einsum("kgts,skd->tkgd", probs, value_all, preferred_element_type=jnp.float32)
    attended = attended.astype(jnp.bfloat16).reshape(tok_rows, -1)
    terms = jnp.dot(attended, wo_attn, preferred_element_type=jnp.float32)
    partial_out = head_reduce_scatter(terms)
    after_window = (hidden_in.astype(jnp.float32) + partial_out).astype(jnp.bfloat16)
    after_whole = head_all_gather(after_window)
    normed2 = norm_rows(after_whole, lin_gain)
    feats = jnp.dot(normed2, w_feature, preferred_element_type=jnp.float32)
    lin_heads = feats.shape[1] // (2 * FEAT)
    feats = feats.reshape(tok_rows, lin_heads, 2, FEAT)
    query_feat = feats[:, :, 0, :]
    key_feat = feats[:, :, 1, :]
    lvalues = (
        jnp.dot(normed2, wv_linear, preferred_element_type=jnp.float32)
        .astype(jnp.bfloat16)
        .reshape(tok_rows, lin_heads, VDIM)
    )
    phi_query = taylor(query_feat)
    phi_key = taylor(key_feat)
    highest = lax.Precision.HIGHEST
    local_state = jnp.einsum(
        "thf,thv->hfv", phi_key, lvalues.astype(jnp.float32), precision=highest
    )
    prior = earlier_sum(local_state)
    carried = entry_state + prior
    cross = jnp.einsum("thf,hfv->thv", phi_query, carried, precision=highest)
    sims = jnp.einsum("thf,shf->hts", query_feat, key_feat, precision=highest) / math.sqrt(FEAT)
    causal = jnp.arange(tok_rows)[:, None] >= jnp.arange(tok_rows)[None, :]
    weights = jnp.where(causal[None], 1.0 + sims + 0.5 * sims * sims, 0.0).astype(jnp.bfloat16)
    intra = jnp.einsum("hts,shv->thv", weights, lvalues, preferred_element_type=jnp.float32)
    lin_out = cross + intra
    scale = lax.rsqrt(jnp.mean(lin_out * lin_out, axis=-1, keepdims=True) + 1e-05)
    lin_normed = (
        (lin_out * scale * out_gain[None]).astype(jnp.bfloat16).reshape(tok_rows, lin_heads * VDIM)
    )
    lin_terms = jnp.dot(lin_normed, wo_linear, preferred_element_type=jnp.float32)
    lin_part = head_reduce_scatter(lin_terms)
    return (after_window.astype(jnp.float32) + lin_part).astype(jnp.bfloat16)


def solution(mesh):
    in_specs = (
        P(("groups", "ctx"), "head"),
        P(),
        P(None, "head"),
        P(None, "head"),
        P(None, "head"),
        P("head", None),
        P(),
        P(None, "head"),
        P(None, "head"),
        P("head", None),
        P("head", None),
        P(("groups", "head"), None, None),
    )
    out_specs = P(("groups", "ctx"), "head")
    return jax.shard_map(body, mesh=mesh, in_specs=in_specs, out_specs=out_specs, check_vma=False)
```

```python
import math

import jax
import jax.numpy as jnp
from jax import lax
from jax.sharding import PartitionSpec as P

HEAD = 128
WINDOW = 64
FEAT = 16
VDIM = 256


def from_behind(value, axis, by):
    devices = lax.axis_size(axis)
    pairs = [(i, i + by) for i in range(devices) if 0 <= i + by < devices]
    return lax.ppermute(value, axis, pairs)


def head_layout():
    devices = lax.axis_size("head")
    return devices, devices // 2


def core_swap(value):
    devices = lax.axis_size("head")
    return lax.ppermute(value, "head", [(h, h ^ 1) for h in range(devices)])


def chip_shift(value, by):
    devices, chips = head_layout()
    pairs = [(h, ((h // 2 + by) % chips) * 2 + h % 2) for h in range(devices)]
    return lax.ppermute(value, "head", pairs)


def head_reduce_scatter(lhs, weight):
    devices, chips = head_layout()
    me = lax.axis_index("head")
    core, chip = me % 2, me // 2
    width = weight.shape[1] // devices

    def block(which, offset):
        col = (((chip + offset) % chips) * 2 + which) * width
        cols = lax.dynamic_slice_in_dim(weight, col, width, axis=1)
        return jnp.dot(lhs, cols, preferred_element_type=jnp.float32)

    order = [chips - 1 - j for j in range(chips)]
    on_chip = {}
    for offset in order:
        on_chip[offset] = block(core, offset) + core_swap(block(1 - core, offset))
    acc = on_chip[chips - 1]
    for step in range(chips - 1):
        got = chip_shift(acc.astype(jnp.bfloat16), 1).astype(jnp.float32)
        acc = got + on_chip[(chips - step - 2) % chips]
    return acc


def head_all_gather(piece):
    rows, cols = piece.shape
    devices, chips = head_layout()
    me = lax.axis_index("head")
    core, chip = me % 2, me // 2
    chip_buf = jnp.zeros((rows, chips, cols), piece.dtype)
    chip_buf = lax.dynamic_update_index_in_dim(chip_buf, piece, chip, axis=1)
    cur = piece
    for step in range(chips - 1):
        cur = chip_shift(cur, 1)
        chip_buf = lax.dynamic_update_index_in_dim(
            chip_buf, cur, (chip + 2 * chips - step - 1) % chips, axis=1
        )
    partner = core_swap(chip_buf)
    whole = jnp.zeros((rows, chips, 2, cols), piece.dtype)
    whole = lax.dynamic_update_index_in_dim(whole, chip_buf, core, axis=2)
    whole = lax.dynamic_update_index_in_dim(whole, partner, 1 - core, axis=2)
    return whole.reshape(rows, devices * cols)


def earlier_sum(local):
    count = lax.axis_size("ctx")
    sent = local.astype(jnp.bfloat16)
    total = jnp.zeros(local.shape, jnp.float32)
    for by in range(1, count):
        pairs = [(i, i + by) for i in range(count - by)]
        total = total + lax.ppermute(sent, "ctx", pairs).astype(jnp.float32)
    return total


def norm_rows(values, gain):
    wide = values.astype(jnp.float32)
    scale = lax.rsqrt(jnp.mean(wide * wide, axis=-1, keepdims=True) + 1e-05)
    return (wide * scale * gain).astype(jnp.bfloat16)


def taylor(inputs):
    width = inputs.shape[-1]
    outer = (inputs[..., :, None] * inputs[..., None, :]).reshape(
        inputs.shape[:-1] + (width * width,)
    )
    ones = jnp.ones(inputs.shape[:-1] + (1,), jnp.float32)
    return jnp.concatenate(
        [ones, inputs / width**0.25, outer / (math.sqrt(2.0) * math.sqrt(width))], axis=-1
    )


CHUNKS = 2


def body(
    hidden_in,
    attn_gain,
    w_query,
    w_keys,
    w_values,
    wo_attn,
    lin_gain,
    w_feature,
    wv_linear,
    out_gain,
    wo_linear,
    entry_state,
):
    tok_rows = hidden_in.shape[0]
    size = tok_rows // CHUNKS
    kv_cols = w_keys.shape[1]
    kv_heads = kv_cols // HEAD
    group = w_query.shape[1] // HEAD // kv_heads
    hidden_parts = [hidden_in[i * size : (i + 1) * size] for i in range(CHUNKS)]

    query_parts, kv_parts = [], []
    for part in hidden_parts:
        normed = norm_rows(head_all_gather(part), attn_gain)
        query_parts.append(
            jnp.dot(normed, w_query, preferred_element_type=jnp.float32).astype(jnp.bfloat16)
        )
        keys = jnp.dot(normed, w_keys, preferred_element_type=jnp.float32).astype(jnp.bfloat16)
        values = jnp.dot(normed, w_values, preferred_element_type=jnp.float32).astype(jnp.bfloat16)
        kv_parts.append(jnp.concatenate([keys, values], axis=1))
    rim = from_behind(kv_parts[-1][size - WINDOW :], "ctx", 1)
    kv_all = jnp.concatenate([rim] + kv_parts, axis=0)
    start = lax.axis_index("ctx") * tok_rows

    after_parts, after_whole_parts = [], []
    for i in range(CHUNKS):
        kv_win = kv_all[i * size : i * size + size + WINDOW]
        key_win = kv_win[:, :kv_cols].reshape(size + WINDOW, kv_heads, HEAD)
        value_win = kv_win[:, kv_cols:].reshape(size + WINDOW, kv_heads, HEAD)
        query_heads = query_parts[i].reshape(size, kv_heads, group, HEAD)
        scores = jnp.einsum(
            "tkgd,skd->kgts", query_heads, key_win, preferred_element_type=jnp.float32
        ) / math.sqrt(HEAD)
        qpos = start + i * size + jnp.arange(size, dtype=jnp.int32)
        kpos = start + i * size - WINDOW + jnp.arange(size + WINDOW, dtype=jnp.int32)
        visible = (
            (kpos[None, :] <= qpos[:, None])
            & (kpos[None, :] > qpos[:, None] - WINDOW)
            & (kpos[None, :] >= 0)
        )
        scores = jnp.where(visible, scores, -jnp.inf)
        top = jnp.max(scores, axis=-1, keepdims=True)
        expd = jnp.exp(scores - top)
        probs = (expd / jnp.sum(expd, axis=-1, keepdims=True)).astype(jnp.bfloat16)
        attended = jnp.einsum(
            "kgts,skd->tkgd", probs, value_win, preferred_element_type=jnp.float32
        )
        attended = attended.astype(jnp.bfloat16).reshape(size, -1)
        partial_out = head_reduce_scatter(attended, wo_attn)
        after_window = (hidden_parts[i].astype(jnp.float32) + partial_out).astype(jnp.bfloat16)
        after_parts.append(after_window)
        after_whole_parts.append(head_all_gather(after_window))

    qf_parts, kf_parts, lv_parts = [], [], []
    for i in range(CHUNKS):
        normed2 = norm_rows(after_whole_parts[i], lin_gain)
        feats = jnp.dot(normed2, w_feature, preferred_element_type=jnp.float32)
        lin_heads = feats.shape[1] // (2 * FEAT)
        feats = feats.reshape(size, lin_heads, 2, FEAT)
        qf_parts.append(feats[:, :, 0, :])
        kf_parts.append(feats[:, :, 1, :])
        lv_parts.append(
            jnp.dot(normed2, wv_linear, preferred_element_type=jnp.float32)
            .astype(jnp.bfloat16)
            .reshape(size, lin_heads, VDIM)
        )
    key_feat = jnp.concatenate(kf_parts, axis=0)
    lvalues = jnp.concatenate(lv_parts, axis=0)
    lin_heads = key_feat.shape[1]
    highest = lax.Precision.HIGHEST
    phi_key = taylor(key_feat)
    local_state = jnp.einsum(
        "thf,thv->hfv", phi_key, lvalues.astype(jnp.float32), precision=highest
    )
    carried = entry_state + earlier_sum(local_state)

    outs = []
    for i in range(CHUNKS):
        query_feat = qf_parts[i]
        phi_query = taylor(query_feat)
        cross = jnp.einsum("thf,hfv->thv", phi_query, carried, precision=highest)
        sims = jnp.einsum(
            "thf,shf->hts", query_feat, key_feat, precision=highest
        ) / math.sqrt(FEAT)
        causal = (i * size + jnp.arange(size))[:, None] >= jnp.arange(tok_rows)[None, :]
        weights = jnp.where(causal[None], 1.0 + sims + 0.5 * sims * sims, 0.0).astype(jnp.bfloat16)
        intra = jnp.einsum("hts,shv->thv", weights, lvalues, preferred_element_type=jnp.float32)
        lin_out = cross + intra
        scale = lax.rsqrt(jnp.mean(lin_out * lin_out, axis=-1, keepdims=True) + 1e-05)
        lin_normed = (
            (lin_out * scale * out_gain[None]).astype(jnp.bfloat16).reshape(size, lin_heads * VDIM)
        )
        lin_part = head_reduce_scatter(lin_normed, wo_linear)
        outs.append((after_parts[i].astype(jnp.float32) + lin_part).astype(jnp.bfloat16))
    return jnp.concatenate(outs, axis=0)


def solution(mesh):
    in_specs = (
        P(("groups", "ctx"), "head"),
        P(),
        P(None, "head"),
        P(None, "head"),
        P(None, "head"),
        P("head", None),
        P(),
        P(None, "head"),
        P(None, "head"),
        P("head", None),
        P("head", None),
        P(("groups", "head"), None, None),
    )
    out_specs = P(("groups", "ctx"), "head")
    return jax.shard_map(body, mesh=mesh, in_specs=in_specs, out_specs=out_specs, check_vma=False)
```

```python
import math

import jax
import jax.numpy as jnp
from jax import lax
from jax.sharding import PartitionSpec as P

HEAD = 128
WINDOW = 64
FEAT = 16
VDIM = 256


def from_behind(value, axis, by):
    devices = lax.axis_size(axis)
    pairs = [(i, i + by) for i in range(devices) if 0 <= i + by < devices]
    return lax.ppermute(value, axis, pairs)


def head_layout():
    devices = lax.axis_size("head")
    return devices, devices // 2


def core_swap(value):
    devices = lax.axis_size("head")
    return lax.ppermute(value, "head", [(h, h ^ 1) for h in range(devices)])


def chip_shift(value, by):
    devices, chips = head_layout()
    pairs = [(h, ((h // 2 + by) % chips) * 2 + h % 2) for h in range(devices)]
    return lax.ppermute(value, "head", pairs)


def head_reduce_scatter(lhs, weight):
    devices, chips = head_layout()
    me = lax.axis_index("head")
    core, chip = me % 2, me // 2
    width = weight.shape[1] // devices

    def block(which, offset):
        col = (((chip + offset) % chips) * 2 + which) * width
        cols = lax.dynamic_slice_in_dim(weight, col, width, axis=1)
        return jnp.dot(lhs, cols, preferred_element_type=jnp.float32)

    order = [chips - 1 - j for j in range(chips)]
    on_chip = {}
    for offset in order:
        on_chip[offset] = block(core, offset) + core_swap(block(1 - core, offset))
    acc = on_chip[chips - 1]
    for step in range(chips - 1):
        got = chip_shift(acc.astype(jnp.bfloat16), 1).astype(jnp.float32)
        acc = got + on_chip[(chips - step - 2) % chips]
    return acc


def gather_sources():
    devices, chips = head_layout()
    me = lax.axis_index("head")
    core, chip = me % 2, me // 2
    ring = [((chip + chips - step - 1) % chips) * 2 for step in range(chips - 1)]
    return [me] + [r + core for r in ring] + [me ^ 1] + [r + 1 - core for r in ring]


def head_all_gather(piece):
    devices, chips = head_layout()
    pieces = [piece, None]
    pieces[1] = core_swap(piece)
    ring, cur = [], piece
    for step in range(chips - 1):
        cur = chip_shift(cur, 1)
        ring.append(cur)
    forwarded = [core_swap(r) for r in ring]
    return jnp.concatenate([piece] + ring + [pieces[1]] + forwarded, axis=1)


def gathered_rows(weight):
    devices, chips = head_layout()
    block = weight.shape[0] // devices
    return jnp.concatenate(
        [lax.dynamic_slice_in_dim(weight, src * block, block, axis=0) for src in gather_sources()],
        axis=0,
    )


def earlier_sum(local):
    count = lax.axis_size("ctx")
    sent = local.astype(jnp.bfloat16)
    total = jnp.zeros(local.shape, jnp.float32)
    for by in range(1, count):
        pairs = [(i, i + by) for i in range(count - by)]
        total = total + lax.ppermute(sent, "ctx", pairs).astype(jnp.float32)
    return total


def norm_rows(values, gain):
    wide = values.astype(jnp.float32)
    scale = lax.rsqrt(jnp.mean(wide * wide, axis=-1, keepdims=True) + 1e-05)
    return (wide * scale * gain).astype(jnp.bfloat16)


def taylor(inputs):
    width = inputs.shape[-1]
    outer = (inputs[..., :, None] * inputs[..., None, :]).reshape(
        inputs.shape[:-1] + (width * width,)
    )
    ones = jnp.ones(inputs.shape[:-1] + (1,), jnp.float32)
    return jnp.concatenate(
        [ones, inputs / width**0.25, outer / (math.sqrt(2.0) * math.sqrt(width))], axis=-1
    )


CHUNKS = 2


def body(
    hidden_in,
    attn_gain,
    w_query,
    w_keys,
    w_values,
    wo_attn,
    lin_gain,
    w_feature,
    wv_linear,
    out_gain,
    wo_linear,
    entry_state,
):
    tok_rows = hidden_in.shape[0]
    size = tok_rows // CHUNKS
    kv_cols = w_keys.shape[1]
    kv_heads = kv_cols // HEAD
    group = w_query.shape[1] // HEAD // kv_heads
    hidden_parts = [hidden_in[i * size : (i + 1) * size] for i in range(CHUNKS)]
    attn_gain = gathered_rows(attn_gain)
    w_query = gathered_rows(w_query)
    w_keys = gathered_rows(w_keys)
    w_values = gathered_rows(w_values)
    lin_gain = gathered_rows(lin_gain)
    w_feature = gathered_rows(w_feature)
    wv_linear = gathered_rows(wv_linear)

    query_parts, kv_parts = [], []
    for part in hidden_parts:
        normed = norm_rows(head_all_gather(part), attn_gain)
        query_parts.append(
            jnp.dot(normed, w_query, preferred_element_type=jnp.float32).astype(jnp.bfloat16)
        )
        keys = jnp.dot(normed, w_keys, preferred_element_type=jnp.float32).astype(jnp.bfloat16)
        values = jnp.dot(normed, w_values, preferred_element_type=jnp.float32).astype(jnp.bfloat16)
        kv_parts.append(jnp.concatenate([keys, values], axis=1))
    rim = from_behind(kv_parts[-1][size - WINDOW :], "ctx", 1)
    kv_all = jnp.concatenate([rim] + kv_parts, axis=0)
    start = lax.axis_index("ctx") * tok_rows

    after_parts, after_whole_parts = [], []
    for i in range(CHUNKS):
        kv_win = kv_all[i * size : i * size + size + WINDOW]
        key_win = kv_win[:, :kv_cols].reshape(size + WINDOW, kv_heads, HEAD)
        value_win = kv_win[:, kv_cols:].reshape(size + WINDOW, kv_heads, HEAD)
        query_heads = query_parts[i].reshape(size, kv_heads, group, HEAD)
        scores = jnp.einsum(
            "tkgd,skd->kgts", query_heads, key_win, preferred_element_type=jnp.float32
        ) / math.sqrt(HEAD)
        qpos = start + i * size + jnp.arange(size, dtype=jnp.int32)
        kpos = start + i * size - WINDOW + jnp.arange(size + WINDOW, dtype=jnp.int32)
        visible = (
            (kpos[None, :] <= qpos[:, None])
            & (kpos[None, :] > qpos[:, None] - WINDOW)
            & (kpos[None, :] >= 0)
        )
        scores = jnp.where(visible, scores, -jnp.inf)
        top = jnp.max(scores, axis=-1, keepdims=True)
        expd = jnp.exp(scores - top)
        probs = (expd / jnp.sum(expd, axis=-1, keepdims=True)).astype(jnp.bfloat16)
        attended = jnp.einsum(
            "kgts,skd->tkgd", probs, value_win, preferred_element_type=jnp.float32
        )
        attended = attended.astype(jnp.bfloat16).reshape(size, -1)
        partial_out = head_reduce_scatter(attended, wo_attn)
        after_window = (hidden_parts[i].astype(jnp.float32) + partial_out).astype(jnp.bfloat16)
        after_parts.append(after_window)
        after_whole_parts.append(head_all_gather(after_window))

    qf_parts, kf_parts, lv_parts = [], [], []
    for i in range(CHUNKS):
        normed2 = norm_rows(after_whole_parts[i], lin_gain)
        feats = jnp.dot(normed2, w_feature, preferred_element_type=jnp.float32)
        lin_heads = feats.shape[1] // (2 * FEAT)
        feats = feats.reshape(size, lin_heads, 2, FEAT)
        qf_parts.append(feats[:, :, 0, :])
        kf_parts.append(feats[:, :, 1, :])
        lv_parts.append(
            jnp.dot(normed2, wv_linear, preferred_element_type=jnp.float32)
            .astype(jnp.bfloat16)
            .reshape(size, lin_heads, VDIM)
        )
    key_feat = jnp.concatenate(kf_parts, axis=0)
    lvalues = jnp.concatenate(lv_parts, axis=0)
    lin_heads = key_feat.shape[1]
    highest = lax.Precision.HIGHEST
    phi_key = taylor(key_feat)
    local_state = jnp.einsum(
        "thf,thv->hfv", phi_key, lvalues.astype(jnp.float32), precision=highest
    )
    carried = entry_state + earlier_sum(local_state)

    outs = []
    for i in range(CHUNKS):
        query_feat = qf_parts[i]
        phi_query = taylor(query_feat)
        cross = jnp.einsum("thf,hfv->thv", phi_query, carried, precision=highest)
        sims = jnp.einsum(
            "thf,shf->hts", query_feat, key_feat, precision=highest
        ) / math.sqrt(FEAT)
        causal = (i * size + jnp.arange(size))[:, None] >= jnp.arange(tok_rows)[None, :]
        weights = jnp.where(causal[None], 1.0 + sims + 0.5 * sims * sims, 0.0).astype(jnp.bfloat16)
        intra = jnp.einsum("hts,shv->thv", weights, lvalues, preferred_element_type=jnp.float32)
        lin_out = cross + intra
        scale = lax.rsqrt(jnp.mean(lin_out * lin_out, axis=-1, keepdims=True) + 1e-05)
        lin_normed = (
            (lin_out * scale * out_gain[None]).astype(jnp.bfloat16).reshape(size, lin_heads * VDIM)
        )
        lin_part = head_reduce_scatter(lin_normed, wo_linear)
        outs.append((after_parts[i].astype(jnp.float32) + lin_part).astype(jnp.bfloat16))
    return jnp.concatenate(outs, axis=0)


def solution(mesh):
    in_specs = (
        P(("groups", "ctx"), "head"),
        P(),
        P(None, "head"),
        P(None, "head"),
        P(None, "head"),
        P("head", None),
        P(),
        P(None, "head"),
        P(None, "head"),
        P("head", None),
        P("head", None),
        P(("groups", "head"), None, None),
    )
    out_specs = P(("groups", "ctx"), "head")
    return jax.shard_map(body, mesh=mesh, in_specs=in_specs, out_specs=out_specs, check_vma=False)
```

```python
import math

import jax
import jax.numpy as jnp
from jax import lax
from jax.sharding import PartitionSpec as P

HEAD = 128
WINDOW = 64
FEAT = 16
VDIM = 256


def from_behind(value, axis, by):
    devices = lax.axis_size(axis)
    pairs = [(i, i + by) for i in range(devices) if 0 <= i + by < devices]
    return lax.ppermute(value, axis, pairs)


def head_layout():
    devices = lax.axis_size("head")
    return devices, devices // 2


def core_swap(value):
    devices = lax.axis_size("head")
    return lax.ppermute(value, "head", [(h, h ^ 1) for h in range(devices)])


LINK = []


def chip_shift(value, by):
    devices, chips = head_layout()
    pairs = [(h, ((h // 2 + by) % chips) * 2 + h % 2) for h in range(devices)]
    if LINK:
        value, _ = lax.optimization_barrier((value, LINK[-1]))
    moved = lax.ppermute(value, "head", pairs)
    LINK.append(moved)
    return moved


def head_reduce_scatter(lhs, weight):
    devices, chips = head_layout()
    me = lax.axis_index("head")
    core, chip = me % 2, me // 2
    width = weight.shape[1] // devices

    def block(which, offset):
        col = (((chip + offset) % chips) * 2 + which) * width
        cols = lax.dynamic_slice_in_dim(weight, col, width, axis=1)
        return jnp.dot(lhs, cols, preferred_element_type=jnp.float32)

    order = [chips - 1 - j for j in range(chips)]
    on_chip = {}
    for offset in order:
        on_chip[offset] = block(core, offset) + core_swap(block(1 - core, offset))
    acc = on_chip[chips - 1]
    for step in range(chips - 1):
        got = chip_shift(acc.astype(jnp.bfloat16), 1).astype(jnp.float32)
        acc = got + on_chip[(chips - step - 2) % chips]
    return acc


def gather_sources():
    devices, chips = head_layout()
    me = lax.axis_index("head")
    core, chip = me % 2, me // 2
    ring = [((chip + chips - step - 1) % chips) * 2 for step in range(chips - 1)]
    return [me] + [r + core for r in ring] + [me ^ 1] + [r + 1 - core for r in ring]


def head_all_gather(piece):
    devices, chips = head_layout()
    pieces = [piece, None]
    pieces[1] = core_swap(piece)
    ring, cur = [], piece
    for step in range(chips - 1):
        cur = chip_shift(cur, 1)
        ring.append(cur)
    forwarded = [core_swap(r) for r in ring]
    return jnp.concatenate([piece] + ring + [pieces[1]] + forwarded, axis=1)


def gathered_rows(weight):
    devices, chips = head_layout()
    block = weight.shape[0] // devices
    return jnp.concatenate(
        [lax.dynamic_slice_in_dim(weight, src * block, block, axis=0) for src in gather_sources()],
        axis=0,
    )


def earlier_sum(local):
    count = lax.axis_size("ctx")
    sent = local.astype(jnp.bfloat16)
    total = jnp.zeros(local.shape, jnp.float32)
    for by in range(1, count):
        pairs = [(i, i + by) for i in range(count - by)]
        total = total + lax.ppermute(sent, "ctx", pairs).astype(jnp.float32)
    return total


def norm_rows(values, gain):
    wide = values.astype(jnp.float32)
    scale = lax.rsqrt(jnp.mean(wide * wide, axis=-1, keepdims=True) + 1e-05)
    return (wide * scale * gain).astype(jnp.bfloat16)


def taylor(inputs):
    width = inputs.shape[-1]
    outer = (inputs[..., :, None] * inputs[..., None, :]).reshape(
        inputs.shape[:-1] + (width * width,)
    )
    ones = jnp.ones(inputs.shape[:-1] + (1,), jnp.float32)
    return jnp.concatenate(
        [ones, inputs / width**0.25, outer / (math.sqrt(2.0) * math.sqrt(width))], axis=-1
    )


CHUNKS = 2


def body(
    hidden_in,
    attn_gain,
    w_query,
    w_keys,
    w_values,
    wo_attn,
    lin_gain,
    w_feature,
    wv_linear,
    out_gain,
    wo_linear,
    entry_state,
):
    LINK.clear()
    tok_rows = hidden_in.shape[0]
    size = tok_rows // CHUNKS
    kv_cols = w_keys.shape[1]
    kv_heads = kv_cols // HEAD
    group = w_query.shape[1] // HEAD // kv_heads
    hidden_parts = [hidden_in[i * size : (i + 1) * size] for i in range(CHUNKS)]
    attn_gain = gathered_rows(attn_gain)
    w_query = gathered_rows(w_query)
    w_keys = gathered_rows(w_keys)
    w_values = gathered_rows(w_values)
    lin_gain = gathered_rows(lin_gain)
    w_feature = gathered_rows(w_feature)
    wv_linear = gathered_rows(wv_linear)

    query_parts, kv_parts = [], []
    for part in hidden_parts:
        normed = norm_rows(head_all_gather(part), attn_gain)
        query_parts.append(
            jnp.dot(normed, w_query, preferred_element_type=jnp.float32).astype(jnp.bfloat16)
        )
        keys = jnp.dot(normed, w_keys, preferred_element_type=jnp.float32).astype(jnp.bfloat16)
        values = jnp.dot(normed, w_values, preferred_element_type=jnp.float32).astype(jnp.bfloat16)
        kv_parts.append(jnp.concatenate([keys, values], axis=1))
    rim = from_behind(kv_parts[-1][size - WINDOW :], "ctx", 1)
    kv_all = jnp.concatenate([rim] + kv_parts, axis=0)
    start = lax.axis_index("ctx") * tok_rows

    partial_parts = [None] * CHUNKS
    for i in reversed(range(CHUNKS)):
        kv_win = kv_all[i * size : i * size + size + WINDOW]
        key_win = kv_win[:, :kv_cols].reshape(size + WINDOW, kv_heads, HEAD)
        value_win = kv_win[:, kv_cols:].reshape(size + WINDOW, kv_heads, HEAD)
        query_heads = query_parts[i].reshape(size, kv_heads, group, HEAD)
        scores = jnp.einsum(
            "tkgd,skd->kgts", query_heads, key_win, preferred_element_type=jnp.float32
        ) / math.sqrt(HEAD)
        qpos = start + i * size + jnp.arange(size, dtype=jnp.int32)
        kpos = start + i * size - WINDOW + jnp.arange(size + WINDOW, dtype=jnp.int32)
        visible = (
            (kpos[None, :] <= qpos[:, None])
            & (kpos[None, :] > qpos[:, None] - WINDOW)
            & (kpos[None, :] >= 0)
        )
        scores = jnp.where(visible, scores, -jnp.inf)
        top = jnp.max(scores, axis=-1, keepdims=True)
        expd = jnp.exp(scores - top)
        probs = (expd / jnp.sum(expd, axis=-1, keepdims=True)).astype(jnp.bfloat16)
        attended = jnp.einsum(
            "kgts,skd->tkgd", probs, value_win, preferred_element_type=jnp.float32
        )
        attended = attended.astype(jnp.bfloat16).reshape(size, -1)
        partial_parts[i] = head_reduce_scatter(attended, wo_attn)
    after_parts, after_whole_parts = [None] * CHUNKS, [None] * CHUNKS
    for i in reversed(range(CHUNKS)):
        after_window = (hidden_parts[i].astype(jnp.float32) + partial_parts[i]).astype(jnp.bfloat16)
        after_parts[i] = after_window
        after_whole_parts[i] = head_all_gather(after_window)

    qf_parts, kf_parts, lv_parts = [], [], []
    for i in range(CHUNKS):
        normed2 = norm_rows(after_whole_parts[i], lin_gain)
        feats = jnp.dot(normed2, w_feature, preferred_element_type=jnp.float32)
        lin_heads = feats.shape[1] // (2 * FEAT)
        feats = feats.reshape(size, lin_heads, 2, FEAT)
        qf_parts.append(feats[:, :, 0, :])
        kf_parts.append(feats[:, :, 1, :])
        lv_parts.append(
            jnp.dot(normed2, wv_linear, preferred_element_type=jnp.float32)
            .astype(jnp.bfloat16)
            .reshape(size, lin_heads, VDIM)
        )
    key_feat = jnp.concatenate(kf_parts, axis=0)
    lvalues = jnp.concatenate(lv_parts, axis=0)
    lin_heads = key_feat.shape[1]
    highest = lax.Precision.HIGHEST
    phi_key = taylor(key_feat)
    local_state = jnp.einsum(
        "thf,thv->hfv", phi_key, lvalues.astype(jnp.float32), precision=highest
    )
    carried = entry_state + earlier_sum(local_state)

    outs = []
    for i in range(CHUNKS):
        query_feat = qf_parts[i]
        phi_query = taylor(query_feat)
        cross = jnp.einsum("thf,hfv->thv", phi_query, carried, precision=highest)
        sims = jnp.einsum(
            "thf,shf->hts", query_feat, key_feat, precision=highest
        ) / math.sqrt(FEAT)
        causal = (i * size + jnp.arange(size))[:, None] >= jnp.arange(tok_rows)[None, :]
        weights = jnp.where(causal[None], 1.0 + sims + 0.5 * sims * sims, 0.0).astype(jnp.bfloat16)
        intra = jnp.einsum("hts,shv->thv", weights, lvalues, preferred_element_type=jnp.float32)
        lin_out = cross + intra
        scale = lax.rsqrt(jnp.mean(lin_out * lin_out, axis=-1, keepdims=True) + 1e-05)
        lin_normed = (
            (lin_out * scale * out_gain[None]).astype(jnp.bfloat16).reshape(size, lin_heads * VDIM)
        )
        lin_part = head_reduce_scatter(lin_normed, wo_linear)
        outs.append((after_parts[i].astype(jnp.float32) + lin_part).astype(jnp.bfloat16))
    return jnp.concatenate(outs, axis=0)


def solution(mesh):
    in_specs = (
        P(("groups", "ctx"), "head"),
        P(),
        P(None, "head"),
        P(None, "head"),
        P(None, "head"),
        P("head", None),
        P(),
        P(None, "head"),
        P(None, "head"),
        P("head", None),
        P("head", None),
        P(("groups", "head"), None, None),
    )
    out_specs = P(("groups", "ctx"), "head")
    return jax.shard_map(body, mesh=mesh, in_specs=in_specs, out_specs=out_specs, check_vma=False)
```

```python
import math

import jax
import jax.numpy as jnp
from jax import lax
from jax.sharding import PartitionSpec as P

HEAD = 128
WINDOW = 64
FEAT = 16
VDIM = 256


def from_behind(value, axis, by):
    devices = lax.axis_size(axis)
    pairs = [(i, i + by) for i in range(devices) if 0 <= i + by < devices]
    return lax.ppermute(value, axis, pairs)


def head_layout():
    devices = lax.axis_size("head")
    return devices, devices // 2


def core_swap(value):
    devices = lax.axis_size("head")
    return lax.ppermute(value, "head", [(h, h ^ 1) for h in range(devices)])


LINK = []


def chip_shift(value, by):
    devices, chips = head_layout()
    pairs = [(h, ((h // 2 + by) % chips) * 2 + h % 2) for h in range(devices)]
    if LINK:
        value, _ = lax.optimization_barrier((value, LINK[-1]))
    moved = lax.ppermute(value, "head", pairs)
    LINK.append(moved)
    return moved


def head_reduce_scatter(lhs, weight):
    devices, chips = head_layout()
    me = lax.axis_index("head")
    core, chip = me % 2, me // 2
    width = weight.shape[1] // devices

    def block(which, offset):
        col = (((chip + offset) % chips) * 2 + which) * width
        cols = lax.dynamic_slice_in_dim(weight, col, width, axis=1)
        return jnp.dot(lhs, cols, preferred_element_type=jnp.float32)

    order = [chips - 1 - j for j in range(chips)]
    on_chip = {}
    for offset in order:
        on_chip[offset] = block(core, offset) + core_swap(block(1 - core, offset))
    acc = on_chip[chips - 1]
    for step in range(chips - 1):
        got = chip_shift(acc.astype(jnp.bfloat16), 1).astype(jnp.float32)
        acc = got + on_chip[(chips - step - 2) % chips]
    return acc


def gather_sources():
    devices, chips = head_layout()
    me = lax.axis_index("head")
    core, chip = me % 2, me // 2
    ring = [((chip + chips - step - 1) % chips) * 2 for step in range(chips - 1)]
    return [me] + [r + core for r in ring] + [me ^ 1] + [r + 1 - core for r in ring]


def head_all_gather(piece):
    devices, chips = head_layout()
    pieces = [piece, None]
    pieces[1] = core_swap(piece)
    ring, cur = [], piece
    for step in range(chips - 1):
        cur = chip_shift(cur, 1)
        ring.append(cur)
    forwarded = [core_swap(r) for r in ring]
    return jnp.concatenate([piece] + ring + [pieces[1]] + forwarded, axis=1)


def gathered_rows(weight):
    devices, chips = head_layout()
    block = weight.shape[0] // devices
    return jnp.concatenate(
        [lax.dynamic_slice_in_dim(weight, src * block, block, axis=0) for src in gather_sources()],
        axis=0,
    )


def earlier_sum(local):
    count = lax.axis_size("ctx")
    sent = local.astype(jnp.bfloat16)
    total = jnp.zeros(local.shape, jnp.float32)
    for by in range(1, count):
        pairs = [(i, i + by) for i in range(count - by)]
        total = total + lax.ppermute(sent, "ctx", pairs).astype(jnp.float32)
    return total


def norm_rows(values, gain):
    wide = values.astype(jnp.float32)
    scale = lax.rsqrt(jnp.mean(wide * wide, axis=-1, keepdims=True) + 1e-05)
    return (wide * scale * gain).astype(jnp.bfloat16)


def taylor(inputs):
    width = inputs.shape[-1]
    outer = (inputs[..., :, None] * inputs[..., None, :]).reshape(
        inputs.shape[:-1] + (width * width,)
    )
    ones = jnp.ones(inputs.shape[:-1] + (1,), jnp.float32)
    return jnp.concatenate(
        [ones, inputs / width**0.25, outer / (math.sqrt(2.0) * math.sqrt(width))], axis=-1
    )


CHUNKS = 2


def body(
    hidden_in,
    attn_gain,
    w_query,
    w_keys,
    w_values,
    wo_attn,
    lin_gain,
    w_feature,
    wv_linear,
    out_gain,
    wo_linear,
    entry_state,
):
    LINK.clear()
    tok_rows = hidden_in.shape[0]
    size = tok_rows // CHUNKS
    kv_cols = w_keys.shape[1]
    kv_heads = kv_cols // HEAD
    group = w_query.shape[1] // HEAD // kv_heads
    hidden_parts = [hidden_in[i * size : (i + 1) * size] for i in range(CHUNKS)]
    attn_gain = gathered_rows(attn_gain)
    w_query = gathered_rows(w_query)
    w_keys = gathered_rows(w_keys)
    w_values = gathered_rows(w_values)
    lin_gain = gathered_rows(lin_gain)
    w_feature = gathered_rows(w_feature)
    wv_linear = gathered_rows(wv_linear)

    tail = from_behind(hidden_in[tok_rows - WINDOW :], "ctx", 1)
    query_parts, kv_parts = [], []
    for i, part in enumerate(hidden_parts):
        if i == 0:
            part = jnp.concatenate([tail, part], axis=0)
        normed = norm_rows(head_all_gather(part), attn_gain)
        query_rows = normed[WINDOW:] if i == 0 else normed
        query_parts.append(
            jnp.dot(query_rows, w_query, preferred_element_type=jnp.float32).astype(jnp.bfloat16)
        )
        keys = jnp.dot(normed, w_keys, preferred_element_type=jnp.float32).astype(jnp.bfloat16)
        values = jnp.dot(normed, w_values, preferred_element_type=jnp.float32).astype(jnp.bfloat16)
        kv_parts.append(jnp.concatenate([keys, values], axis=1))
    kv_all = jnp.concatenate(kv_parts, axis=0)
    start = lax.axis_index("ctx") * tok_rows

    partial_parts = [None] * CHUNKS
    for i in range(CHUNKS):
        kv_win = kv_all[i * size : i * size + size + WINDOW]
        key_win = kv_win[:, :kv_cols].reshape(size + WINDOW, kv_heads, HEAD)
        value_win = kv_win[:, kv_cols:].reshape(size + WINDOW, kv_heads, HEAD)
        query_heads = query_parts[i].reshape(size, kv_heads, group, HEAD)
        scores = jnp.einsum(
            "tkgd,skd->kgts", query_heads, key_win, preferred_element_type=jnp.float32
        ) / math.sqrt(HEAD)
        qpos = start + i * size + jnp.arange(size, dtype=jnp.int32)
        kpos = start + i * size - WINDOW + jnp.arange(size + WINDOW, dtype=jnp.int32)
        visible = (
            (kpos[None, :] <= qpos[:, None])
            & (kpos[None, :] > qpos[:, None] - WINDOW)
            & (kpos[None, :] >= 0)
        )
        scores = jnp.where(visible, scores, -jnp.inf)
        top = jnp.max(scores, axis=-1, keepdims=True)
        expd = jnp.exp(scores - top)
        probs = (expd / jnp.sum(expd, axis=-1, keepdims=True)).astype(jnp.bfloat16)
        attended = jnp.einsum(
            "kgts,skd->tkgd", probs, value_win, preferred_element_type=jnp.float32
        )
        attended = attended.astype(jnp.bfloat16).reshape(size, -1)
        partial_parts[i] = head_reduce_scatter(attended, wo_attn)
    after_parts, after_whole_parts = [None] * CHUNKS, [None] * CHUNKS
    for i in range(CHUNKS):
        after_window = (hidden_parts[i].astype(jnp.float32) + partial_parts[i]).astype(jnp.bfloat16)
        after_parts[i] = after_window
        after_whole_parts[i] = head_all_gather(after_window)

    qf_parts, kf_parts, lv_parts = [], [], []
    for i in range(CHUNKS):
        normed2 = norm_rows(after_whole_parts[i], lin_gain)
        feats = jnp.dot(normed2, w_feature, preferred_element_type=jnp.float32)
        lin_heads = feats.shape[1] // (2 * FEAT)
        feats = feats.reshape(size, lin_heads, 2, FEAT)
        qf_parts.append(feats[:, :, 0, :])
        kf_parts.append(feats[:, :, 1, :])
        lv_parts.append(
            jnp.dot(normed2, wv_linear, preferred_element_type=jnp.float32)
            .astype(jnp.bfloat16)
            .reshape(size, lin_heads, VDIM)
        )
    key_feat = jnp.concatenate(kf_parts, axis=0)
    lvalues = jnp.concatenate(lv_parts, axis=0)
    lin_heads = key_feat.shape[1]
    highest = lax.Precision.HIGHEST
    phi_key = taylor(key_feat)
    local_state = jnp.einsum(
        "thf,thv->hfv", phi_key, lvalues.astype(jnp.float32), precision=highest
    )
    carried = entry_state + earlier_sum(local_state)

    outs = []
    for i in range(CHUNKS):
        query_feat = qf_parts[i]
        phi_query = taylor(query_feat)
        cross = jnp.einsum("thf,hfv->thv", phi_query, carried, precision=highest)
        sims = jnp.einsum(
            "thf,shf->hts", query_feat, key_feat, precision=highest
        ) / math.sqrt(FEAT)
        causal = (i * size + jnp.arange(size))[:, None] >= jnp.arange(tok_rows)[None, :]
        weights = jnp.where(causal[None], 1.0 + sims + 0.5 * sims * sims, 0.0).astype(jnp.bfloat16)
        intra = jnp.einsum("hts,shv->thv", weights, lvalues, preferred_element_type=jnp.float32)
        lin_out = cross + intra
        scale = lax.rsqrt(jnp.mean(lin_out * lin_out, axis=-1, keepdims=True) + 1e-05)
        lin_normed = (
            (lin_out * scale * out_gain[None]).astype(jnp.bfloat16).reshape(size, lin_heads * VDIM)
        )
        lin_part = head_reduce_scatter(lin_normed, wo_linear)
        outs.append((after_parts[i].astype(jnp.float32) + lin_part).astype(jnp.bfloat16))
    return jnp.concatenate(outs, axis=0)


def solution(mesh):
    in_specs = (
        P(("groups", "ctx"), "head"),
        P(),
        P(None, "head"),
        P(None, "head"),
        P(None, "head"),
        P("head", None),
        P(),
        P(None, "head"),
        P(None, "head"),
        P("head", None),
        P("head", None),
        P(("groups", "head"), None, None),
    )
    out_specs = P(("groups", "ctx"), "head")
    return jax.shard_map(body, mesh=mesh, in_specs=in_specs, out_specs=out_specs, check_vma=False)
```

```python
import math

import jax
import jax.numpy as jnp
from jax import lax
from jax.sharding import PartitionSpec as P

HEAD = 128
WINDOW = 64
FEAT = 16
VDIM = 256


def from_behind(value, axis, by):
    devices = lax.axis_size(axis)
    pairs = [(i, i + by) for i in range(devices) if 0 <= i + by < devices]
    return lax.ppermute(value, axis, pairs)


def head_layout():
    devices = lax.axis_size("head")
    return devices, devices // 2


def core_swap(value):
    devices = lax.axis_size("head")
    return lax.ppermute(value, "head", [(h, h ^ 1) for h in range(devices)])


def chip_shift(value, by):
    devices, chips = head_layout()
    pairs = [(h, ((h // 2 + by) % chips) * 2 + h % 2) for h in range(devices)]
    return lax.ppermute(value, "head", pairs)


def head_reduce_scatter(lhs, weight):
    devices, chips = head_layout()
    me = lax.axis_index("head")
    core, chip = me % 2, me // 2
    width = weight.shape[1] // devices

    def block(which, offset):
        col = (((chip + offset) % chips) * 2 + which) * width
        cols = lax.dynamic_slice_in_dim(weight, col, width, axis=1)
        return jnp.dot(lhs, cols, preferred_element_type=jnp.float32)

    order = [chips - 1 - j for j in range(chips)]
    on_chip = {}
    for offset in order:
        on_chip[offset] = block(core, offset) + core_swap(block(1 - core, offset))
    acc = on_chip[chips - 1]
    for step in range(chips - 1):
        got = chip_shift(acc.astype(jnp.bfloat16), 1).astype(jnp.float32)
        acc = got + on_chip[(chips - step - 2) % chips]
    return acc


def gather_sources():
    devices, chips = head_layout()
    me = lax.axis_index("head")
    core, chip = me % 2, me // 2
    ring = [((chip + chips - step - 1) % chips) * 2 for step in range(chips - 1)]
    return [me] + [r + core for r in ring] + [me ^ 1] + [r + 1 - core for r in ring]


def head_all_gather(piece):
    devices, chips = head_layout()
    pieces = [piece, None]
    pieces[1] = core_swap(piece)
    ring, cur = [], piece
    for step in range(chips - 1):
        cur = chip_shift(cur, 1)
        ring.append(cur)
    forwarded = [core_swap(r) for r in ring]
    return jnp.concatenate([piece] + ring + [pieces[1]] + forwarded, axis=1)


def gathered_rows(weight):
    devices, chips = head_layout()
    block = weight.shape[0] // devices
    return jnp.concatenate(
        [lax.dynamic_slice_in_dim(weight, src * block, block, axis=0) for src in gather_sources()],
        axis=0,
    )


def earlier_sum(local):
    count = lax.axis_size("ctx")
    sent = local.astype(jnp.bfloat16)
    total = jnp.zeros(local.shape, jnp.float32)
    for by in range(1, count):
        pairs = [(i, i + by) for i in range(count - by)]
        total = total + lax.ppermute(sent, "ctx", pairs).astype(jnp.float32)
    return total


def norm_rows(values, gain):
    wide = values.astype(jnp.float32)
    scale = lax.rsqrt(jnp.mean(wide * wide, axis=-1, keepdims=True) + 1e-05)
    return (wide * scale * gain).astype(jnp.bfloat16)


def taylor(inputs):
    width = inputs.shape[-1]
    outer = (inputs[..., :, None] * inputs[..., None, :]).reshape(
        inputs.shape[:-1] + (width * width,)
    )
    ones = jnp.ones(inputs.shape[:-1] + (1,), jnp.float32)
    return jnp.concatenate(
        [ones, inputs / width**0.25, outer / (math.sqrt(2.0) * math.sqrt(width))], axis=-1
    )


CHUNKS = 1


def body(
    hidden_in,
    attn_gain,
    w_query,
    w_keys,
    w_values,
    wo_attn,
    lin_gain,
    w_feature,
    wv_linear,
    out_gain,
    wo_linear,
    entry_state,
):
    tok_rows = hidden_in.shape[0]
    size = tok_rows // CHUNKS
    kv_cols = w_keys.shape[1]
    kv_heads = kv_cols // HEAD
    group = w_query.shape[1] // HEAD // kv_heads
    hidden_parts = [hidden_in[i * size : (i + 1) * size] for i in range(CHUNKS)]
    attn_gain = gathered_rows(attn_gain)
    w_query = gathered_rows(w_query)
    w_keys = gathered_rows(w_keys)
    w_values = gathered_rows(w_values)
    lin_gain = gathered_rows(lin_gain)
    w_feature = gathered_rows(w_feature)
    wv_linear = gathered_rows(wv_linear)

    query_parts, kv_parts = [], []
    for part in hidden_parts:
        normed = norm_rows(head_all_gather(part), attn_gain)
        query_parts.append(
            jnp.dot(normed, w_query, preferred_element_type=jnp.float32).astype(jnp.bfloat16)
        )
        keys = jnp.dot(normed, w_keys, preferred_element_type=jnp.float32).astype(jnp.bfloat16)
        values = jnp.dot(normed, w_values, preferred_element_type=jnp.float32).astype(jnp.bfloat16)
        kv_parts.append(jnp.concatenate([keys, values], axis=1))
    rim = from_behind(kv_parts[-1][size - WINDOW :], "ctx", 1)
    kv_all = jnp.concatenate([rim] + kv_parts, axis=0)
    start = lax.axis_index("ctx") * tok_rows

    after_parts, after_whole_parts = [], []
    for i in range(CHUNKS):
        kv_win = kv_all[i * size : i * size + size + WINDOW]
        key_win = kv_win[:, :kv_cols].reshape(size + WINDOW, kv_heads, HEAD)
        value_win = kv_win[:, kv_cols:].reshape(size + WINDOW, kv_heads, HEAD)
        query_heads = query_parts[i].reshape(size, kv_heads, group, HEAD)
        scores = jnp.einsum(
            "tkgd,skd->kgts", query_heads, key_win, preferred_element_type=jnp.float32
        ) / math.sqrt(HEAD)
        qpos = start + i * size + jnp.arange(size, dtype=jnp.int32)
        kpos = start + i * size - WINDOW + jnp.arange(size + WINDOW, dtype=jnp.int32)
        visible = (
            (kpos[None, :] <= qpos[:, None])
            & (kpos[None, :] > qpos[:, None] - WINDOW)
            & (kpos[None, :] >= 0)
        )
        scores = jnp.where(visible, scores, -jnp.inf)
        top = jnp.max(scores, axis=-1, keepdims=True)
        expd = jnp.exp(scores - top)
        probs = (expd / jnp.sum(expd, axis=-1, keepdims=True)).astype(jnp.bfloat16)
        attended = jnp.einsum(
            "kgts,skd->tkgd", probs, value_win, preferred_element_type=jnp.float32
        )
        attended = attended.astype(jnp.bfloat16).reshape(size, -1)
        partial_out = head_reduce_scatter(attended, wo_attn)
        after_window = (hidden_parts[i].astype(jnp.float32) + partial_out).astype(jnp.bfloat16)
        after_parts.append(after_window)
        after_whole_parts.append(head_all_gather(after_window))

    qf_parts, kf_parts, lv_parts = [], [], []
    for i in range(CHUNKS):
        normed2 = norm_rows(after_whole_parts[i], lin_gain)
        feats = jnp.dot(normed2, w_feature, preferred_element_type=jnp.float32)
        lin_heads = feats.shape[1] // (2 * FEAT)
        feats = feats.reshape(size, lin_heads, 2, FEAT)
        qf_parts.append(feats[:, :, 0, :])
        kf_parts.append(feats[:, :, 1, :])
        lv_parts.append(
            jnp.dot(normed2, wv_linear, preferred_element_type=jnp.float32)
            .astype(jnp.bfloat16)
            .reshape(size, lin_heads, VDIM)
        )
    key_feat = jnp.concatenate(kf_parts, axis=0)
    lvalues = jnp.concatenate(lv_parts, axis=0)
    lin_heads = key_feat.shape[1]
    highest = lax.Precision.HIGHEST
    phi_key = taylor(key_feat)
    local_state = jnp.einsum(
        "thf,thv->hfv", phi_key, lvalues.astype(jnp.float32), precision=highest
    )
    carried = entry_state + earlier_sum(local_state)

    outs = []
    for i in range(CHUNKS):
        query_feat = qf_parts[i]
        phi_query = taylor(query_feat)
        cross = jnp.einsum("thf,hfv->thv", phi_query, carried, precision=highest)
        sims = jnp.einsum(
            "thf,shf->hts", query_feat, key_feat, precision=highest
        ) / math.sqrt(FEAT)
        causal = (i * size + jnp.arange(size))[:, None] >= jnp.arange(tok_rows)[None, :]
        weights = jnp.where(causal[None], 1.0 + sims + 0.5 * sims * sims, 0.0).astype(jnp.bfloat16)
        intra = jnp.einsum("hts,shv->thv", weights, lvalues, preferred_element_type=jnp.float32)
        lin_out = cross + intra
        scale = lax.rsqrt(jnp.mean(lin_out * lin_out, axis=-1, keepdims=True) + 1e-05)
        lin_normed = (
            (lin_out * scale * out_gain[None]).astype(jnp.bfloat16).reshape(size, lin_heads * VDIM)
        )
        lin_part = head_reduce_scatter(lin_normed, wo_linear)
        outs.append((after_parts[i].astype(jnp.float32) + lin_part).astype(jnp.bfloat16))
    return jnp.concatenate(outs, axis=0)


def solution(mesh):
    in_specs = (
        P(("groups", "ctx"), "head"),
        P(),
        P(None, "head"),
        P(None, "head"),
        P(None, "head"),
        P("head", None),
        P(),
        P(None, "head"),
        P(None, "head"),
        P("head", None),
        P("head", None),
        P(("groups", "head"), None, None),
    )
    out_specs = P(("groups", "ctx"), "head")
    return jax.shard_map(body, mesh=mesh, in_specs=in_specs, out_specs=out_specs, check_vma=False)
```

```python
import math

import jax
import jax.numpy as jnp
from jax import lax
from jax.sharding import PartitionSpec as P

HEAD = 128
WINDOW = 64
FEAT = 16
VDIM = 256


def from_behind(value, axis, by):
    devices = lax.axis_size(axis)
    pairs = [(i, i + by) for i in range(devices) if 0 <= i + by < devices]
    return lax.ppermute(value, axis, pairs)


def head_layout():
    devices = lax.axis_size("head")
    return devices, devices // 2


def core_swap(value):
    devices = lax.axis_size("head")
    return lax.ppermute(value, "head", [(h, h ^ 1) for h in range(devices)])


LINK = []


def chip_shift(value, by):
    devices, chips = head_layout()
    pairs = [(h, ((h // 2 + by) % chips) * 2 + h % 2) for h in range(devices)]
    if LINK:
        value, _ = lax.optimization_barrier((value, LINK[-1]))
    moved = lax.ppermute(value, "head", pairs)
    LINK.append(moved)
    return moved


def after(value, dep):
    if dep is None:
        return value
    value, _ = lax.optimization_barrier((value, dep))
    return value


def head_reduce_scatter(lhs, weight, dep=None):
    devices, chips = head_layout()
    me = lax.axis_index("head")
    core, chip = me % 2, me // 2
    width = weight.shape[1] // devices

    def block(which, offset):
        col = (((chip + offset) % chips) * 2 + which) * width
        cols = lax.dynamic_slice_in_dim(weight, col, width, axis=1)
        return jnp.dot(lhs, cols, preferred_element_type=jnp.float32)

    order = [chips - 1 - j for j in range(chips)]
    on_chip = {}
    for offset in order:
        on_chip[offset] = block(core, offset) + core_swap(block(1 - core, offset))
    acc = on_chip[chips - 1]
    for step in range(chips - 1):
        got = after(chip_shift(acc.astype(jnp.bfloat16), 1), dep).astype(jnp.float32)
        acc = got + on_chip[(chips - step - 2) % chips]
    return acc


def gather_sources():
    devices, chips = head_layout()
    me = lax.axis_index("head")
    core, chip = me % 2, me // 2
    ring = [((chip + chips - step - 1) % chips) * 2 for step in range(chips - 1)]
    return [me] + [r + core for r in ring] + [me ^ 1] + [r + 1 - core for r in ring]


def gather_start(piece):
    devices, chips = head_layout()
    ring, cur = [], piece
    for step in range(chips - 1):
        cur = chip_shift(cur, 1)
        ring.append(cur)
    return piece, core_swap(piece), ring


def gather_finish(started, dep=None):
    piece, partner, ring = started
    forwarded = [core_swap(after(r, dep)) for r in ring]
    return jnp.concatenate([piece] + ring + [partner] + forwarded, axis=1)


def head_all_gather(piece, dep=None):
    return gather_finish(gather_start(piece), dep)


def gathered_rows(weight):
    devices, chips = head_layout()
    block = weight.shape[0] // devices
    return jnp.concatenate(
        [lax.dynamic_slice_in_dim(weight, src * block, block, axis=0) for src in gather_sources()],
        axis=0,
    )


def earlier_sum(local):
    count = lax.axis_size("ctx")
    sent = local.astype(jnp.bfloat16)
    total = jnp.zeros(local.shape, jnp.float32)
    for by in range(1, count):
        pairs = [(i, i + by) for i in range(count - by)]
        total = total + lax.ppermute(sent, "ctx", pairs).astype(jnp.float32)
    return total


def norm_rows(values, gain):
    wide = values.astype(jnp.float32)
    scale = lax.rsqrt(jnp.mean(wide * wide, axis=-1, keepdims=True) + 1e-05)
    return (wide * scale * gain).astype(jnp.bfloat16)


def taylor(inputs):
    width = inputs.shape[-1]
    outer = (inputs[..., :, None] * inputs[..., None, :]).reshape(
        inputs.shape[:-1] + (width * width,)
    )
    ones = jnp.ones(inputs.shape[:-1] + (1,), jnp.float32)
    return jnp.concatenate(
        [ones, inputs / width**0.25, outer / (math.sqrt(2.0) * math.sqrt(width))], axis=-1
    )


CHUNKS = 2


def body(
    hidden_in,
    attn_gain,
    w_query,
    w_keys,
    w_values,
    wo_attn,
    lin_gain,
    w_feature,
    wv_linear,
    out_gain,
    wo_linear,
    entry_state,
):
    LINK.clear()
    tok_rows = hidden_in.shape[0]
    size = tok_rows // CHUNKS
    kv_cols = w_keys.shape[1]
    kv_heads = kv_cols // HEAD
    group = w_query.shape[1] // HEAD // kv_heads
    hidden_parts = [hidden_in[i * size : (i + 1) * size] for i in range(CHUNKS)]
    attn_gain = gathered_rows(attn_gain)
    w_query = gathered_rows(w_query)
    w_keys = gathered_rows(w_keys)
    w_values = gathered_rows(w_values)
    lin_gain = gathered_rows(lin_gain)
    w_feature = gathered_rows(w_feature)
    wv_linear = gathered_rows(wv_linear)

    tail = from_behind(hidden_in[tok_rows - WINDOW :], "ctx", 1)
    parts = [jnp.concatenate([tail, hidden_parts[0]], axis=0)] + hidden_parts[1:]
    start = lax.axis_index("ctx") * tok_rows

    def project(whole, first):
        normed = norm_rows(whole, attn_gain)
        query_rows = normed[WINDOW:] if first else normed
        query = jnp.dot(query_rows, w_query, preferred_element_type=jnp.float32).astype(jnp.bfloat16)
        keys = jnp.dot(normed, w_keys, preferred_element_type=jnp.float32).astype(jnp.bfloat16)
        values = jnp.dot(normed, w_values, preferred_element_type=jnp.float32).astype(jnp.bfloat16)
        return query, jnp.concatenate([keys, values], axis=1)

    def attend(i, query, kv_win):
        key_win = kv_win[:, :kv_cols].reshape(size + WINDOW, kv_heads, HEAD)
        value_win = kv_win[:, kv_cols:].reshape(size + WINDOW, kv_heads, HEAD)
        query_heads = query.reshape(size, kv_heads, group, HEAD)
        scores = jnp.einsum(
            "tkgd,skd->kgts", query_heads, key_win, preferred_element_type=jnp.float32
        ) / math.sqrt(HEAD)
        qpos = start + i * size + jnp.arange(size, dtype=jnp.int32)
        kpos = start + i * size - WINDOW + jnp.arange(size + WINDOW, dtype=jnp.int32)
        visible = (
            (kpos[None, :] <= qpos[:, None])
            & (kpos[None, :] > qpos[:, None] - WINDOW)
            & (kpos[None, :] >= 0)
        )
        scores = jnp.where(visible, scores, -jnp.inf)
        top = jnp.max(scores, axis=-1, keepdims=True)
        expd = jnp.exp(scores - top)
        probs = (expd / jnp.sum(expd, axis=-1, keepdims=True)).astype(jnp.bfloat16)
        attended = jnp.einsum(
            "kgts,skd->tkgd", probs, value_win, preferred_element_type=jnp.float32
        )
        return attended.astype(jnp.bfloat16).reshape(size, -1)

    started = [gather_start(parts[0])]
    wholes = [gather_finish(started[0])]
    kv_parts, attended_parts = [], []
    for i in range(CHUNKS):
        if i + 1 < CHUNKS:
            started.append(gather_start(parts[i + 1]))
        query, kv = project(wholes[i], i == 0)
        kv_parts.append(kv)
        if i == 0:
            kv_win = kv
        else:
            kv_win = jnp.concatenate([kv_parts[i - 1][-WINDOW:], kv], axis=0)
        attended_parts.append(attend(i, query, kv_win))
        if i + 1 < CHUNKS:
            wholes.append(gather_finish(started[i + 1], attended_parts[i]))

    after_parts = [None] * CHUNKS
    qf_parts, kf_parts, lv_parts = [], [], []
    dep = attended_parts[1] if CHUNKS > 1 else None
    for i in range(CHUNKS):
        partial = head_reduce_scatter(attended_parts[i], wo_attn, dep)
        after_parts[i] = (hidden_parts[i].astype(jnp.float32) + partial).astype(jnp.bfloat16)
        normed2 = norm_rows(head_all_gather(after_parts[i]), lin_gain)
        feats = jnp.dot(normed2, w_feature, preferred_element_type=jnp.float32)
        lin_heads = feats.shape[1] // (2 * FEAT)
        feats = feats.reshape(size, lin_heads, 2, FEAT)
        qf_parts.append(feats[:, :, 0, :])
        kf_parts.append(feats[:, :, 1, :])
        lv_parts.append(
            jnp.dot(normed2, wv_linear, preferred_element_type=jnp.float32)
            .astype(jnp.bfloat16)
            .reshape(size, lin_heads, VDIM)
        )
        dep = lv_parts[-1]
    key_feat = jnp.concatenate(kf_parts, axis=0)
    lvalues = jnp.concatenate(lv_parts, axis=0)
    lin_heads = key_feat.shape[1]
    highest = lax.Precision.HIGHEST
    phi_key = taylor(key_feat)
    local_state = jnp.einsum(
        "thf,thv->hfv", phi_key, lvalues.astype(jnp.float32), precision=highest
    )
    carried = entry_state + earlier_sum(local_state)

    normed_parts = []
    for i in range(CHUNKS):
        query_feat = qf_parts[i]
        phi_query = taylor(query_feat)
        cross = jnp.einsum("thf,hfv->thv", phi_query, carried, precision=highest)
        sims = jnp.einsum(
            "thf,shf->hts", query_feat, key_feat, precision=highest
        ) / math.sqrt(FEAT)
        causal = (i * size + jnp.arange(size))[:, None] >= jnp.arange(tok_rows)[None, :]
        weights = jnp.where(causal[None], 1.0 + sims + 0.5 * sims * sims, 0.0).astype(jnp.bfloat16)
        intra = jnp.einsum("hts,shv->thv", weights, lvalues, preferred_element_type=jnp.float32)
        lin_out = cross + intra
        scale = lax.rsqrt(jnp.mean(lin_out * lin_out, axis=-1, keepdims=True) + 1e-05)
        normed_parts.append(
            (lin_out * scale * out_gain[None]).astype(jnp.bfloat16).reshape(size, lin_heads * VDIM)
        )
    outs = []
    for i in range(CHUNKS):
        dep = normed_parts[i + 1] if i + 1 < CHUNKS else None
        lin_part = head_reduce_scatter(normed_parts[i], wo_linear, dep)
        outs.append((after_parts[i].astype(jnp.float32) + lin_part).astype(jnp.bfloat16))
    return jnp.concatenate(outs, axis=0)


def solution(mesh):
    in_specs = (
        P(("groups", "ctx"), "head"),
        P(),
        P(None, "head"),
        P(None, "head"),
        P(None, "head"),
        P("head", None),
        P(),
        P(None, "head"),
        P(None, "head"),
        P("head", None),
        P("head", None),
        P(("groups", "head"), None, None),
    )
    out_specs = P(("groups", "ctx"), "head")
    return jax.shard_map(body, mesh=mesh, in_specs=in_specs, out_specs=out_specs, check_vma=False)
```

```python
import math

import jax
import jax.numpy as jnp
from jax import lax
from jax.sharding import PartitionSpec as P

HEAD = 128
WINDOW = 64
FEAT = 16
VDIM = 256


def from_behind(value, axis, by):
    devices = lax.axis_size(axis)
    pairs = [(i, i + by) for i in range(devices) if 0 <= i + by < devices]
    return lax.ppermute(value, axis, pairs)


def head_layout():
    devices = lax.axis_size("head")
    return devices, devices // 2


def core_swap(value):
    devices = lax.axis_size("head")
    return lax.ppermute(value, "head", [(h, h ^ 1) for h in range(devices)])


LINK = []


def chip_shift(value, by):
    devices, chips = head_layout()
    pairs = [(h, ((h // 2 + by) % chips) * 2 + h % 2) for h in range(devices)]
    if LINK:
        value, _ = lax.optimization_barrier((value, LINK[-1]))
    moved = lax.ppermute(value, "head", pairs)
    LINK.append(moved)
    return moved


def after(value, dep):
    if dep is None:
        return value
    value, _ = lax.optimization_barrier((value, dep))
    return value


def head_reduce_scatter(lhs, weight, dep=None):
    devices, chips = head_layout()
    me = lax.axis_index("head")
    core, chip = me % 2, me // 2
    width = weight.shape[1] // devices

    def block(which, offset):
        col = (((chip + offset) % chips) * 2 + which) * width
        cols = lax.dynamic_slice_in_dim(weight, col, width, axis=1)
        return jnp.dot(lhs, cols, preferred_element_type=jnp.float32)

    order = [chips - 1 - j for j in range(chips)]
    on_chip = {}
    for offset in order:
        on_chip[offset] = block(core, offset) + core_swap(block(1 - core, offset))
    acc = on_chip[chips - 1]
    for step in range(chips - 1):
        got = after(chip_shift(acc.astype(jnp.bfloat16), 1), dep).astype(jnp.float32)
        acc = got + on_chip[(chips - step - 2) % chips]
    return acc


def gather_sources():
    devices, chips = head_layout()
    me = lax.axis_index("head")
    core, chip = me % 2, me // 2
    ring = [((chip + chips - step - 1) % chips) * 2 for step in range(chips - 1)]
    return [me] + [r + core for r in ring] + [me ^ 1] + [r + 1 - core for r in ring]


def gather_start(piece):
    devices, chips = head_layout()
    ring, cur = [], piece
    for step in range(chips - 1):
        cur = chip_shift(cur, 1)
        ring.append(cur)
    return piece, core_swap(piece), ring


def gather_finish(started, dep=None):
    piece, partner, ring = started
    forwarded = [core_swap(after(r, dep)) for r in ring]
    return jnp.concatenate([piece] + ring + [partner] + forwarded, axis=1)


def head_all_gather(piece, dep=None):
    return gather_finish(gather_start(piece), dep)


def gathered_rows(weight):
    devices, chips = head_layout()
    block = weight.shape[0] // devices
    return jnp.concatenate(
        [lax.dynamic_slice_in_dim(weight, src * block, block, axis=0) for src in gather_sources()],
        axis=0,
    )


def earlier_sum(local):
    count = lax.axis_size("ctx")
    sent = local.astype(jnp.bfloat16)
    total = jnp.zeros(local.shape, jnp.float32)
    for by in range(1, count):
        pairs = [(i, i + by) for i in range(count - by)]
        total = total + lax.ppermute(sent, "ctx", pairs).astype(jnp.float32)
    return total


def norm_rows(values, gain):
    wide = values.astype(jnp.float32)
    scale = lax.rsqrt(jnp.mean(wide * wide, axis=-1, keepdims=True) + 1e-05)
    return (wide * scale * gain).astype(jnp.bfloat16)


def taylor(inputs):
    width = inputs.shape[-1]
    outer = (inputs[..., :, None] * inputs[..., None, :]).reshape(
        inputs.shape[:-1] + (width * width,)
    )
    ones = jnp.ones(inputs.shape[:-1] + (1,), jnp.float32)
    return jnp.concatenate(
        [ones, inputs / width**0.25, outer / (math.sqrt(2.0) * math.sqrt(width))], axis=-1
    )


CHUNKS = 2


def body(
    hidden_in,
    attn_gain,
    w_query,
    w_keys,
    w_values,
    wo_attn,
    lin_gain,
    w_feature,
    wv_linear,
    out_gain,
    wo_linear,
    entry_state,
):
    LINK.clear()
    tok_rows = hidden_in.shape[0]
    size = tok_rows // CHUNKS
    kv_cols = w_keys.shape[1]
    kv_heads = kv_cols // HEAD
    group = w_query.shape[1] // HEAD // kv_heads
    hidden_parts = [hidden_in[i * size : (i + 1) * size] for i in range(CHUNKS)]
    attn_gain = gathered_rows(attn_gain)
    w_query = gathered_rows(w_query)
    w_keys = gathered_rows(w_keys)
    w_values = gathered_rows(w_values)
    lin_gain = gathered_rows(lin_gain)
    w_feature = gathered_rows(w_feature)
    wv_linear = gathered_rows(wv_linear)

    tail = from_behind(hidden_in[tok_rows - WINDOW :], "ctx", 1)
    parts = [jnp.concatenate([tail, hidden_parts[0]], axis=0)] + hidden_parts[1:]
    start = lax.axis_index("ctx") * tok_rows

    def project(whole, first):
        normed = norm_rows(whole, attn_gain)
        query_rows = normed[WINDOW:] if first else normed
        query = jnp.dot(query_rows, w_query, preferred_element_type=jnp.float32).astype(jnp.bfloat16)
        keys = jnp.dot(normed, w_keys, preferred_element_type=jnp.float32).astype(jnp.bfloat16)
        values = jnp.dot(normed, w_values, preferred_element_type=jnp.float32).astype(jnp.bfloat16)
        return query, jnp.concatenate([keys, values], axis=1)

    def attend(i, query, kv_win):
        key_win = kv_win[:, :kv_cols].reshape(size + WINDOW, kv_heads, HEAD)
        value_win = kv_win[:, kv_cols:].reshape(size + WINDOW, kv_heads, HEAD)
        query_heads = query.reshape(size, kv_heads, group, HEAD)
        scores = jnp.einsum(
            "tkgd,skd->kgts", query_heads, key_win, preferred_element_type=jnp.float32
        ) / math.sqrt(HEAD)
        qpos = start + i * size + jnp.arange(size, dtype=jnp.int32)
        kpos = start + i * size - WINDOW + jnp.arange(size + WINDOW, dtype=jnp.int32)
        visible = (
            (kpos[None, :] <= qpos[:, None])
            & (kpos[None, :] > qpos[:, None] - WINDOW)
            & (kpos[None, :] >= 0)
        )
        scores = jnp.where(visible, scores, -jnp.inf)
        top = jnp.max(scores, axis=-1, keepdims=True)
        expd = jnp.exp(scores - top)
        probs = (expd / jnp.sum(expd, axis=-1, keepdims=True)).astype(jnp.bfloat16)
        attended = jnp.einsum(
            "kgts,skd->tkgd", probs, value_win, preferred_element_type=jnp.float32
        )
        return attended.astype(jnp.bfloat16).reshape(size, -1)

    started = [gather_start(parts[0])]
    wholes = [gather_finish(started[0])]
    kv_parts, attended_parts = [], []
    for i in range(CHUNKS):
        if i + 1 < CHUNKS:
            started.append(gather_start(parts[i + 1]))
        query, kv = project(wholes[i], i == 0)
        kv_parts.append(kv)
        if i == 0:
            kv_win = kv
        else:
            kv_win = jnp.concatenate([kv_parts[i - 1][-WINDOW:], kv], axis=0)
        attended_parts.append(attend(i, query, kv_win))
        if i + 1 < CHUNKS:
            wholes.append(gather_finish(started[i + 1], attended_parts[i]))

    after_parts = []
    for i in range(CHUNKS):
        dep = attended_parts[i + 1] if i + 1 < CHUNKS else None
        partial = head_reduce_scatter(attended_parts[i], wo_attn, dep)
        after_parts.append((hidden_parts[i].astype(jnp.float32) + partial).astype(jnp.bfloat16))
    after_window = jnp.concatenate(after_parts, axis=0)

    normed2 = norm_rows(head_all_gather(after_window), lin_gain)
    feats = jnp.dot(normed2, w_feature, preferred_element_type=jnp.float32)
    lin_heads = feats.shape[1] // (2 * FEAT)
    feats = feats.reshape(tok_rows, lin_heads, 2, FEAT)
    query_feat = feats[:, :, 0, :]
    key_feat = feats[:, :, 1, :]
    lvalues = (
        jnp.dot(normed2, wv_linear, preferred_element_type=jnp.float32)
        .astype(jnp.bfloat16)
        .reshape(tok_rows, lin_heads, VDIM)
    )
    highest = lax.Precision.HIGHEST
    phi_key = taylor(key_feat)
    local_state = jnp.einsum(
        "thf,thv->hfv", phi_key, lvalues.astype(jnp.float32), precision=highest
    )
    prior = earlier_sum(local_state)
    phi_query = taylor(query_feat)
    sims = jnp.einsum("thf,shf->hts", query_feat, key_feat, precision=highest) / math.sqrt(FEAT)
    causal = jnp.arange(tok_rows)[:, None] >= jnp.arange(tok_rows)[None, :]
    weights = jnp.where(causal[None], 1.0 + sims + 0.5 * sims * sims, 0.0).astype(jnp.bfloat16)
    intra = jnp.einsum("hts,shv->thv", weights, lvalues, preferred_element_type=jnp.float32)
    own = jnp.einsum("thf,hfv->thv", phi_query, entry_state, precision=highest) + intra
    lin_out = own + jnp.einsum("thf,hfv->thv", phi_query, prior, precision=highest)
    scale = lax.rsqrt(jnp.mean(lin_out * lin_out, axis=-1, keepdims=True) + 1e-05)
    lin_normed = (
        (lin_out * scale * out_gain[None]).astype(jnp.bfloat16).reshape(tok_rows, lin_heads * VDIM)
    )
    lin_part = head_reduce_scatter(lin_normed, wo_linear)
    return (after_window.astype(jnp.float32) + lin_part).astype(jnp.bfloat16)


def solution(mesh):
    in_specs = (
        P(("groups", "ctx"), "head"),
        P(),
        P(None, "head"),
        P(None, "head"),
        P(None, "head"),
        P("head", None),
        P(),
        P(None, "head"),
        P(None, "head"),
        P("head", None),
        P("head", None),
        P(("groups", "head"), None, None),
    )
    out_specs = P(("groups", "ctx"), "head")
    return jax.shard_map(body, mesh=mesh, in_specs=in_specs, out_specs=out_specs, check_vma=False)
```

```python
import math

import jax
import jax.numpy as jnp
from jax import lax
from jax.sharding import PartitionSpec as P

HEAD = 128
WINDOW = 64
FEAT = 16
VDIM = 256


def from_behind(value, axis, by):
    devices = lax.axis_size(axis)
    pairs = [(i, i + by) for i in range(devices) if 0 <= i + by < devices]
    return lax.ppermute(value, axis, pairs)


def head_layout():
    devices = lax.axis_size("head")
    return devices, devices // 2


def core_swap(value):
    devices = lax.axis_size("head")
    return lax.ppermute(value, "head", [(h, h ^ 1) for h in range(devices)])


def chip_shift(value, by):
    devices, chips = head_layout()
    pairs = [(h, ((h // 2 + by) % chips) * 2 + h % 2) for h in range(devices)]
    return lax.ppermute(value, "head", pairs)


def after(value, dep):
    value, _ = lax.optimization_barrier((value, dep))
    return value


def head_reduce_scatter(lhs, weight):
    devices, chips = head_layout()
    me = lax.axis_index("head")
    core, chip = me % 2, me // 2
    width = weight.shape[1] // devices

    def on_chip_sum(source, offset):
        sums = []
        for which in (core, 1 - core):
            col = (((chip + offset) % chips) * 2 + which) * width
            cols = lax.dynamic_slice_in_dim(weight, col, width, axis=1)
            sums.append(jnp.dot(source, cols, preferred_element_type=jnp.float32))
        return sums[0] + core_swap(sums[1])

    acc = on_chip_sum(lhs, chips - 1)
    for step in range(chips - 1):
        sent = acc.astype(jnp.bfloat16)
        got = chip_shift(sent, 1).astype(jnp.float32)
        acc = got + on_chip_sum(after(lhs, sent), (chips - step - 2) % chips)
    return acc


def gather_sources():
    devices, chips = head_layout()
    me = lax.axis_index("head")
    core, chip = me % 2, me // 2
    ring = [((chip + chips - step - 1) % chips) * 2 for step in range(chips - 1)]
    return [me] + [r + core for r in ring] + [me ^ 1] + [r + 1 - core for r in ring]


def head_all_gather(piece):
    devices, chips = head_layout()
    pieces = [piece, None]
    pieces[1] = core_swap(piece)
    ring, cur = [], piece
    for step in range(chips - 1):
        cur = chip_shift(cur, 1)
        ring.append(cur)
    forwarded = [core_swap(r) for r in ring]
    return jnp.concatenate([piece] + ring + [pieces[1]] + forwarded, axis=1)


def gathered_rows(weight):
    devices, chips = head_layout()
    block = weight.shape[0] // devices
    return jnp.concatenate(
        [lax.dynamic_slice_in_dim(weight, src * block, block, axis=0) for src in gather_sources()],
        axis=0,
    )


def earlier_sum(local):
    count = lax.axis_size("ctx")
    sent = local.astype(jnp.bfloat16)
    total = jnp.zeros(local.shape, jnp.float32)
    for by in range(1, count):
        pairs = [(i, i + by) for i in range(count - by)]
        total = total + lax.ppermute(sent, "ctx", pairs).astype(jnp.float32)
    return total


def norm_rows(values, gain):
    wide = values.astype(jnp.float32)
    scale = lax.rsqrt(jnp.mean(wide * wide, axis=-1, keepdims=True) + 1e-05)
    return (wide * scale * gain).astype(jnp.bfloat16)


def taylor(inputs):
    width = inputs.shape[-1]
    outer = (inputs[..., :, None] * inputs[..., None, :]).reshape(
        inputs.shape[:-1] + (width * width,)
    )
    ones = jnp.ones(inputs.shape[:-1] + (1,), jnp.float32)
    return jnp.concatenate(
        [ones, inputs / width**0.25, outer / (math.sqrt(2.0) * math.sqrt(width))], axis=-1
    )


CHUNKS = 1


def body(
    hidden_in,
    attn_gain,
    w_query,
    w_keys,
    w_values,
    wo_attn,
    lin_gain,
    w_feature,
    wv_linear,
    out_gain,
    wo_linear,
    entry_state,
):
    tok_rows = hidden_in.shape[0]
    size = tok_rows // CHUNKS
    kv_cols = w_keys.shape[1]
    kv_heads = kv_cols // HEAD
    group = w_query.shape[1] // HEAD // kv_heads
    hidden_parts = [hidden_in[i * size : (i + 1) * size] for i in range(CHUNKS)]
    attn_gain = gathered_rows(attn_gain)
    w_query = gathered_rows(w_query)
    w_keys = gathered_rows(w_keys)
    w_values = gathered_rows(w_values)
    lin_gain = gathered_rows(lin_gain)
    w_feature = gathered_rows(w_feature)
    wv_linear = gathered_rows(wv_linear)

    query_parts, kv_parts = [], []
    for part in hidden_parts:
        normed = norm_rows(head_all_gather(part), attn_gain)
        query_parts.append(
            jnp.dot(normed, w_query, preferred_element_type=jnp.float32).astype(jnp.bfloat16)
        )
        keys = jnp.dot(normed, w_keys, preferred_element_type=jnp.float32).astype(jnp.bfloat16)
        values = jnp.dot(normed, w_values, preferred_element_type=jnp.float32).astype(jnp.bfloat16)
        kv_parts.append(jnp.concatenate([keys, values], axis=1))
    rim = from_behind(kv_parts[-1][size - WINDOW :], "ctx", 1)
    kv_all = jnp.concatenate([rim] + kv_parts, axis=0)
    start = lax.axis_index("ctx") * tok_rows

    after_parts, after_whole_parts = [], []
    for i in range(CHUNKS):
        kv_win = kv_all[i * size : i * size + size + WINDOW]
        key_win = kv_win[:, :kv_cols].reshape(size + WINDOW, kv_heads, HEAD)
        value_win = kv_win[:, kv_cols:].reshape(size + WINDOW, kv_heads, HEAD)
        query_heads = query_parts[i].reshape(size, kv_heads, group, HEAD)
        scores = jnp.einsum(
            "tkgd,skd->kgts", query_heads, key_win, preferred_element_type=jnp.float32
        ) / math.sqrt(HEAD)
        qpos = start + i * size + jnp.arange(size, dtype=jnp.int32)
        kpos = start + i * size - WINDOW + jnp.arange(size + WINDOW, dtype=jnp.int32)
        visible = (
            (kpos[None, :] <= qpos[:, None])
            & (kpos[None, :] > qpos[:, None] - WINDOW)
            & (kpos[None, :] >= 0)
        )
        scores = jnp.where(visible, scores, -jnp.inf)
        top = jnp.max(scores, axis=-1, keepdims=True)
        expd = jnp.exp(scores - top)
        probs = (expd / jnp.sum(expd, axis=-1, keepdims=True)).astype(jnp.bfloat16)
        attended = jnp.einsum(
            "kgts,skd->tkgd", probs, value_win, preferred_element_type=jnp.float32
        )
        attended = attended.astype(jnp.bfloat16).reshape(size, -1)
        partial_out = head_reduce_scatter(attended, wo_attn)
        after_window = (hidden_parts[i].astype(jnp.float32) + partial_out).astype(jnp.bfloat16)
        after_parts.append(after_window)
        after_whole_parts.append(head_all_gather(after_window))

    qf_parts, kf_parts, lv_parts = [], [], []
    for i in range(CHUNKS):
        normed2 = norm_rows(after_whole_parts[i], lin_gain)
        feats = jnp.dot(normed2, w_feature, preferred_element_type=jnp.float32)
        lin_heads = feats.shape[1] // (2 * FEAT)
        feats = feats.reshape(size, lin_heads, 2, FEAT)
        qf_parts.append(feats[:, :, 0, :])
        kf_parts.append(feats[:, :, 1, :])
        lv_parts.append(
            jnp.dot(normed2, wv_linear, preferred_element_type=jnp.float32)
            .astype(jnp.bfloat16)
            .reshape(size, lin_heads, VDIM)
        )
    key_feat = jnp.concatenate(kf_parts, axis=0)
    lvalues = jnp.concatenate(lv_parts, axis=0)
    lin_heads = key_feat.shape[1]
    highest = lax.Precision.HIGHEST
    phi_key = taylor(key_feat)
    local_state = jnp.einsum(
        "thf,thv->hfv", phi_key, lvalues.astype(jnp.float32), precision=highest
    )
    carried = entry_state + earlier_sum(local_state)

    outs = []
    for i in range(CHUNKS):
        query_feat = qf_parts[i]
        phi_query = taylor(query_feat)
        cross = jnp.einsum("thf,hfv->thv", phi_query, carried, precision=highest)
        sims = jnp.einsum(
            "thf,shf->hts", query_feat, key_feat, precision=highest
        ) / math.sqrt(FEAT)
        causal = (i * size + jnp.arange(size))[:, None] >= jnp.arange(tok_rows)[None, :]
        weights = jnp.where(causal[None], 1.0 + sims + 0.5 * sims * sims, 0.0).astype(jnp.bfloat16)
        intra = jnp.einsum("hts,shv->thv", weights, lvalues, preferred_element_type=jnp.float32)
        lin_out = cross + intra
        scale = lax.rsqrt(jnp.mean(lin_out * lin_out, axis=-1, keepdims=True) + 1e-05)
        lin_normed = (
            (lin_out * scale * out_gain[None]).astype(jnp.bfloat16).reshape(size, lin_heads * VDIM)
        )
        lin_part = head_reduce_scatter(lin_normed, wo_linear)
        outs.append((after_parts[i].astype(jnp.float32) + lin_part).astype(jnp.bfloat16))
    return jnp.concatenate(outs, axis=0)


def solution(mesh):
    in_specs = (
        P(("groups", "ctx"), "head"),
        P(),
        P(None, "head"),
        P(None, "head"),
        P(None, "head"),
        P("head", None),
        P(),
        P(None, "head"),
        P(None, "head"),
        P("head", None),
        P("head", None),
        P(("groups", "head"), None, None),
    )
    out_specs = P(("groups", "ctx"), "head")
    return jax.shard_map(body, mesh=mesh, in_specs=in_specs, out_specs=out_specs, check_vma=False)
```

```python
import math

import jax
import jax.numpy as jnp
from jax import lax
from jax.sharding import PartitionSpec as P

HEAD = 128
WINDOW = 64
FEAT = 16
VDIM = 256


def from_behind(value, axis, by):
    devices = lax.axis_size(axis)
    pairs = [(i, i + by) for i in range(devices) if 0 <= i + by < devices]
    return lax.ppermute(value, axis, pairs)


def head_layout():
    devices = lax.axis_size("head")
    return devices, devices // 2


def core_swap(value):
    devices = lax.axis_size("head")
    return lax.ppermute(value, "head", [(h, h ^ 1) for h in range(devices)])


def chip_shift(value, by):
    devices, chips = head_layout()
    pairs = [(h, ((h // 2 + by) % chips) * 2 + h % 2) for h in range(devices)]
    return lax.ppermute(value, "head", pairs)


def head_reduce_scatter(lhs, weight):
    devices, chips = head_layout()
    me = lax.axis_index("head")
    core, chip = me % 2, me // 2
    width = weight.shape[1] // devices

    def block(which, offset):
        col = (((chip + offset) % chips) * 2 + which) * width
        cols = lax.dynamic_slice_in_dim(weight, col, width, axis=1)
        return jnp.dot(lhs, cols, preferred_element_type=jnp.float32)

    order = [chips - 1 - j for j in range(chips)]
    on_chip = {}
    for offset in order:
        on_chip[offset] = block(core, offset) + core_swap(block(1 - core, offset))
    acc = on_chip[chips - 1]
    for step in range(chips - 1):
        got = chip_shift(acc.astype(jnp.bfloat16), 1).astype(jnp.float32)
        acc = got + on_chip[(chips - step - 2) % chips]
    return acc


def gather_sources():
    devices, chips = head_layout()
    me = lax.axis_index("head")
    core, chip = me % 2, me // 2
    ring = [((chip + chips - step - 1) % chips) * 2 for step in range(chips - 1)]
    return [me] + [r + core for r in ring] + [me ^ 1] + [r + 1 - core for r in ring]


def head_all_gather(piece):
    devices, chips = head_layout()
    pieces = [piece, None]
    pieces[1] = core_swap(piece)
    ring, cur = [], piece
    for step in range(chips - 1):
        cur = chip_shift(cur, 1)
        ring.append(cur)
    forwarded = [core_swap(r) for r in ring]
    return jnp.concatenate([piece] + ring + [pieces[1]] + forwarded, axis=1)


def gathered_rows(weight):
    devices, chips = head_layout()
    block = weight.shape[0] // devices
    return jnp.concatenate(
        [lax.dynamic_slice_in_dim(weight, src * block, block, axis=0) for src in gather_sources()],
        axis=0,
    )


def earlier_sum(local):
    count = lax.axis_size("ctx")
    sent = local.astype(jnp.bfloat16)
    total = jnp.zeros(local.shape, jnp.float32)
    for by in range(1, count):
        pairs = [(i, i + by) for i in range(count - by)]
        total = total + lax.ppermute(sent, "ctx", pairs).astype(jnp.float32)
    return total


def norm_rows(values, gain):
    wide = values.astype(jnp.float32)
    scale = lax.rsqrt(jnp.mean(wide * wide, axis=-1, keepdims=True) + 1e-05)
    return (wide * scale * gain).astype(jnp.bfloat16)


def taylor(inputs):
    width = inputs.shape[-1]
    outer = (inputs[..., :, None] * inputs[..., None, :]).reshape(
        inputs.shape[:-1] + (width * width,)
    )
    ones = jnp.ones(inputs.shape[:-1] + (1,), jnp.float32)
    return jnp.concatenate(
        [ones, inputs / width**0.25, outer / (math.sqrt(2.0) * math.sqrt(width))], axis=-1
    )


CHUNKS = 1


def body(
    hidden_in,
    attn_gain,
    w_query,
    w_keys,
    w_values,
    wo_attn,
    lin_gain,
    w_feature,
    wv_linear,
    out_gain,
    wo_linear,
    entry_state,
):
    tok_rows = hidden_in.shape[0]
    size = tok_rows // CHUNKS
    kv_cols = w_keys.shape[1]
    kv_heads = kv_cols // HEAD
    group = w_query.shape[1] // HEAD // kv_heads
    hidden_parts = [hidden_in[i * size : (i + 1) * size] for i in range(CHUNKS)]
    attn_gain = gathered_rows(attn_gain)
    w_query = gathered_rows(w_query)
    w_keys = gathered_rows(w_keys)
    w_values = gathered_rows(w_values)
    lin_gain = gathered_rows(lin_gain)
    w_feature = gathered_rows(w_feature)
    wv_linear = gathered_rows(wv_linear)

    query_parts, kv_parts = [], []
    for part in hidden_parts:
        normed = norm_rows(head_all_gather(part), attn_gain)
        query_parts.append(
            jnp.dot(normed, w_query, preferred_element_type=jnp.float32).astype(jnp.bfloat16)
        )
        keys = jnp.dot(normed, w_keys, preferred_element_type=jnp.float32).astype(jnp.bfloat16)
        values = jnp.dot(normed, w_values, preferred_element_type=jnp.float32).astype(jnp.bfloat16)
        kv_parts.append(jnp.concatenate([keys, values], axis=1))
    rim = from_behind(kv_parts[-1][size - WINDOW :], "ctx", 1)
    kv_all = jnp.concatenate([rim] + kv_parts, axis=0)
    start = lax.axis_index("ctx") * tok_rows

    after_parts, after_whole_parts = [], []
    for i in range(CHUNKS):
        kv_win = kv_all[i * size : i * size + size + WINDOW]
        blocks = size // WINDOW
        kv_blocks = jnp.concatenate(
            [
                kv_win[:-WINDOW].reshape(blocks, WINDOW, 2 * kv_cols),
                kv_win[WINDOW:].reshape(blocks, WINDOW, 2 * kv_cols),
            ],
            axis=1,
        )
        key_blocks = kv_blocks[..., :kv_cols].reshape(blocks, 2 * WINDOW, kv_heads, HEAD)
        value_blocks = kv_blocks[..., kv_cols:].reshape(blocks, 2 * WINDOW, kv_heads, HEAD)
        query_blocks = query_parts[i].reshape(blocks, WINDOW, kv_heads, group, HEAD)
        scores = jnp.einsum(
            "bqkgd,bskd->bkgqs", query_blocks, key_blocks, preferred_element_type=jnp.float32
        ) / math.sqrt(HEAD)
        base = start + i * size + WINDOW * jnp.arange(blocks, dtype=jnp.int32)
        qpos = base[:, None] + jnp.arange(WINDOW, dtype=jnp.int32)[None, :]
        kpos = base[:, None] - WINDOW + jnp.arange(2 * WINDOW, dtype=jnp.int32)[None, :]
        visible = (
            (kpos[:, None, :] <= qpos[:, :, None])
            & (kpos[:, None, :] > qpos[:, :, None] - WINDOW)
            & (kpos[:, None, :] >= 0)
        )
        scores = jnp.where(visible[:, None, None], scores, -jnp.inf)
        top = jnp.max(scores, axis=-1, keepdims=True)
        expd = jnp.exp(scores - top)
        probs = (expd / jnp.sum(expd, axis=-1, keepdims=True)).astype(jnp.bfloat16)
        attended = jnp.einsum(
            "bkgqs,bskd->bqkgd", probs, value_blocks, preferred_element_type=jnp.float32
        )
        attended = attended.astype(jnp.bfloat16).reshape(size, -1)
        partial_out = head_reduce_scatter(attended, wo_attn)
        after_window = (hidden_parts[i].astype(jnp.float32) + partial_out).astype(jnp.bfloat16)
        after_parts.append(after_window)
        after_whole_parts.append(head_all_gather(after_window))

    qf_parts, kf_parts, lv_parts = [], [], []
    for i in range(CHUNKS):
        normed2 = norm_rows(after_whole_parts[i], lin_gain)
        feats = jnp.dot(normed2, w_feature, preferred_element_type=jnp.float32)
        lin_heads = feats.shape[1] // (2 * FEAT)
        feats = feats.reshape(size, lin_heads, 2, FEAT)
        qf_parts.append(feats[:, :, 0, :])
        kf_parts.append(feats[:, :, 1, :])
        lv_parts.append(
            jnp.dot(normed2, wv_linear, preferred_element_type=jnp.float32)
            .astype(jnp.bfloat16)
            .reshape(size, lin_heads, VDIM)
        )
    key_feat = jnp.concatenate(kf_parts, axis=0)
    lvalues = jnp.concatenate(lv_parts, axis=0)
    lin_heads = key_feat.shape[1]
    highest = lax.Precision.HIGHEST
    phi_key = taylor(key_feat)
    local_state = jnp.einsum(
        "thf,thv->hfv", phi_key, lvalues.astype(jnp.float32), precision=highest
    )
    carried = entry_state + earlier_sum(local_state)

    outs = []
    for i in range(CHUNKS):
        query_feat = qf_parts[i]
        phi_query = taylor(query_feat)
        cross = jnp.einsum("thf,hfv->thv", phi_query, carried, precision=highest)
        sims = jnp.einsum(
            "thf,shf->hts", query_feat, key_feat, precision=highest
        ) / math.sqrt(FEAT)
        causal = (i * size + jnp.arange(size))[:, None] >= jnp.arange(tok_rows)[None, :]
        weights = jnp.where(causal[None], 1.0 + sims + 0.5 * sims * sims, 0.0).astype(jnp.bfloat16)
        intra = jnp.einsum("hts,shv->thv", weights, lvalues, preferred_element_type=jnp.float32)
        lin_out = cross + intra
        scale = lax.rsqrt(jnp.mean(lin_out * lin_out, axis=-1, keepdims=True) + 1e-05)
        lin_normed = (
            (lin_out * scale * out_gain[None]).astype(jnp.bfloat16).reshape(size, lin_heads * VDIM)
        )
        lin_part = head_reduce_scatter(lin_normed, wo_linear)
        outs.append((after_parts[i].astype(jnp.float32) + lin_part).astype(jnp.bfloat16))
    return jnp.concatenate(outs, axis=0)


def solution(mesh):
    in_specs = (
        P(("groups", "ctx"), "head"),
        P(),
        P(None, "head"),
        P(None, "head"),
        P(None, "head"),
        P("head", None),
        P(),
        P(None, "head"),
        P(None, "head"),
        P("head", None),
        P("head", None),
        P(("groups", "head"), None, None),
    )
    out_specs = P(("groups", "ctx"), "head")
    return jax.shard_map(body, mesh=mesh, in_specs=in_specs, out_specs=out_specs, check_vma=False)
```

```python
import math

import jax
import jax.numpy as jnp
from jax import lax
from jax.sharding import PartitionSpec as P

HEAD = 128
WINDOW = 64
FEAT = 16
VDIM = 256


def from_behind(value, axis, by):
    devices = lax.axis_size(axis)
    pairs = [(i, i + by) for i in range(devices) if 0 <= i + by < devices]
    return lax.ppermute(value, axis, pairs)


def head_layout():
    devices = lax.axis_size("head")
    return devices, devices // 2


def core_swap(value):
    devices = lax.axis_size("head")
    return lax.ppermute(value, "head", [(h, h ^ 1) for h in range(devices)])


def chip_shift(value, by):
    devices, chips = head_layout()
    pairs = [(h, ((h // 2 + by) % chips) * 2 + h % 2) for h in range(devices)]
    return lax.ppermute(value, "head", pairs)


def head_reduce_scatter(lhs, weight):
    devices, chips = head_layout()
    me = lax.axis_index("head")
    core, chip = me % 2, me // 2
    width = weight.shape[1] // devices

    def block(which, offset):
        col = (((chip + offset) % chips) * 2 + which) * width
        cols = lax.dynamic_slice_in_dim(weight, col, width, axis=1)
        return jnp.dot(lhs, cols, preferred_element_type=jnp.float32)

    order = [chips - 1 - j for j in range(chips)]
    on_chip = {}
    for offset in order:
        on_chip[offset] = block(core, offset) + core_swap(block(1 - core, offset))
    acc = on_chip[chips - 1]
    for step in range(chips - 1):
        got = chip_shift(acc.astype(jnp.bfloat16), 1).astype(jnp.float32)
        acc = got + on_chip[(chips - step - 2) % chips]
    return acc


def residual_exchange(lhs, weight, whole, piece):
    devices, chips = head_layout()
    me = lax.axis_index("head")
    core, chip = me % 2, me // 2
    width = weight.shape[1] // devices

    def on_chip_sum(offset):
        sums = []
        for which in (core, 1 - core):
            col = (((chip + offset) % chips) * 2 + which) * width
            cols = lax.dynamic_slice_in_dim(weight, col, width, axis=1)
            sums.append(jnp.dot(lhs, cols, preferred_element_type=jnp.float32))
        return sums[0] + core_swap(sums[1])

    there, here = on_chip_sum(1), on_chip_sum(0)
    sent = jnp.concatenate([there, here], axis=1).astype(jnp.bfloat16)
    got = chip_shift(sent, 1).astype(jnp.float32)
    mine = (piece.astype(jnp.float32) + here + got[:, :width]).astype(jnp.bfloat16)
    other = (whole[:, width : 2 * width].astype(jnp.float32) + there + got[:, width:]).astype(
        jnp.bfloat16
    )
    pair = jnp.concatenate([mine, other], axis=1)
    return mine, jnp.concatenate([pair, core_swap(pair)], axis=1)


def gather_sources():
    devices, chips = head_layout()
    me = lax.axis_index("head")
    core, chip = me % 2, me // 2
    ring = [((chip + chips - step - 1) % chips) * 2 for step in range(chips - 1)]
    return [me] + [r + core for r in ring] + [me ^ 1] + [r + 1 - core for r in ring]


def head_all_gather(piece):
    devices, chips = head_layout()
    pieces = [piece, None]
    pieces[1] = core_swap(piece)
    ring, cur = [], piece
    for step in range(chips - 1):
        cur = chip_shift(cur, 1)
        ring.append(cur)
    forwarded = [core_swap(r) for r in ring]
    return jnp.concatenate([piece] + ring + [pieces[1]] + forwarded, axis=1)


def gathered_rows(weight):
    devices, chips = head_layout()
    block = weight.shape[0] // devices
    return jnp.concatenate(
        [lax.dynamic_slice_in_dim(weight, src * block, block, axis=0) for src in gather_sources()],
        axis=0,
    )


def earlier_sum(local):
    count = lax.axis_size("ctx")
    sent = local.astype(jnp.bfloat16)
    total = jnp.zeros(local.shape, jnp.float32)
    for by in range(1, count):
        pairs = [(i, i + by) for i in range(count - by)]
        total = total + lax.ppermute(sent, "ctx", pairs).astype(jnp.float32)
    return total


def norm_rows(values, gain):
    wide = values.astype(jnp.float32)
    scale = lax.rsqrt(jnp.mean(wide * wide, axis=-1, keepdims=True) + 1e-05)
    return (wide * scale * gain).astype(jnp.bfloat16)


def taylor(inputs):
    width = inputs.shape[-1]
    outer = (inputs[..., :, None] * inputs[..., None, :]).reshape(
        inputs.shape[:-1] + (width * width,)
    )
    ones = jnp.ones(inputs.shape[:-1] + (1,), jnp.float32)
    return jnp.concatenate(
        [ones, inputs / width**0.25, outer / (math.sqrt(2.0) * math.sqrt(width))], axis=-1
    )


CHUNKS = 1


def body(
    hidden_in,
    attn_gain,
    w_query,
    w_keys,
    w_values,
    wo_attn,
    lin_gain,
    w_feature,
    wv_linear,
    out_gain,
    wo_linear,
    entry_state,
):
    tok_rows = hidden_in.shape[0]
    size = tok_rows // CHUNKS
    kv_cols = w_keys.shape[1]
    kv_heads = kv_cols // HEAD
    group = w_query.shape[1] // HEAD // kv_heads
    hidden_parts = [hidden_in[i * size : (i + 1) * size] for i in range(CHUNKS)]
    attn_gain = gathered_rows(attn_gain)
    w_query = gathered_rows(w_query)
    w_keys = gathered_rows(w_keys)
    w_values = gathered_rows(w_values)
    lin_gain = gathered_rows(lin_gain)
    w_feature = gathered_rows(w_feature)
    wv_linear = gathered_rows(wv_linear)

    query_parts, kv_parts = [], []
    hidden_wholes = []
    for part in hidden_parts:
        hidden_wholes.append(head_all_gather(part))
        normed = norm_rows(hidden_wholes[-1], attn_gain)
        query_parts.append(
            jnp.dot(normed, w_query, preferred_element_type=jnp.float32).astype(jnp.bfloat16)
        )
        keys = jnp.dot(normed, w_keys, preferred_element_type=jnp.float32).astype(jnp.bfloat16)
        values = jnp.dot(normed, w_values, preferred_element_type=jnp.float32).astype(jnp.bfloat16)
        kv_parts.append(jnp.concatenate([keys, values], axis=1))
    rim = from_behind(kv_parts[-1][size - WINDOW :], "ctx", 1)
    kv_all = jnp.concatenate([rim] + kv_parts, axis=0)
    start = lax.axis_index("ctx") * tok_rows

    after_parts, after_whole_parts = [], []
    for i in range(CHUNKS):
        kv_win = kv_all[i * size : i * size + size + WINDOW]
        key_win = kv_win[:, :kv_cols].reshape(size + WINDOW, kv_heads, HEAD)
        value_win = kv_win[:, kv_cols:].reshape(size + WINDOW, kv_heads, HEAD)
        query_heads = query_parts[i].reshape(size, kv_heads, group, HEAD)
        scores = jnp.einsum(
            "tkgd,skd->kgts", query_heads, key_win, preferred_element_type=jnp.float32
        ) / math.sqrt(HEAD)
        qpos = start + i * size + jnp.arange(size, dtype=jnp.int32)
        kpos = start + i * size - WINDOW + jnp.arange(size + WINDOW, dtype=jnp.int32)
        visible = (
            (kpos[None, :] <= qpos[:, None])
            & (kpos[None, :] > qpos[:, None] - WINDOW)
            & (kpos[None, :] >= 0)
        )
        scores = jnp.where(visible, scores, -jnp.inf)
        top = jnp.max(scores, axis=-1, keepdims=True)
        expd = jnp.exp(scores - top)
        probs = (expd / jnp.sum(expd, axis=-1, keepdims=True)).astype(jnp.bfloat16)
        attended = jnp.einsum(
            "kgts,skd->tkgd", probs, value_win, preferred_element_type=jnp.float32
        )
        attended = attended.astype(jnp.bfloat16).reshape(size, -1)
        if head_layout()[1] == 2:
            after_window, after_whole = residual_exchange(
                attended, wo_attn, hidden_wholes[i], hidden_parts[i]
            )
        else:
            partial_out = head_reduce_scatter(attended, wo_attn)
            after_window = (hidden_parts[i].astype(jnp.float32) + partial_out).astype(jnp.bfloat16)
            after_whole = head_all_gather(after_window)
        after_parts.append(after_window)
        after_whole_parts.append(after_whole)

    qf_parts, kf_parts, lv_parts = [], [], []
    for i in range(CHUNKS):
        normed2 = norm_rows(after_whole_parts[i], lin_gain)
        feats = jnp.dot(normed2, w_feature, preferred_element_type=jnp.float32)
        lin_heads = feats.shape[1] // (2 * FEAT)
        feats = feats.reshape(size, lin_heads, 2, FEAT)
        qf_parts.append(feats[:, :, 0, :])
        kf_parts.append(feats[:, :, 1, :])
        lv_parts.append(
            jnp.dot(normed2, wv_linear, preferred_element_type=jnp.float32)
            .astype(jnp.bfloat16)
            .reshape(size, lin_heads, VDIM)
        )
    key_feat = jnp.concatenate(kf_parts, axis=0)
    lvalues = jnp.concatenate(lv_parts, axis=0)
    lin_heads = key_feat.shape[1]
    highest = lax.Precision.HIGHEST
    phi_key = taylor(key_feat)
    local_state = jnp.einsum(
        "thf,thv->hfv", phi_key, lvalues.astype(jnp.float32), precision=highest
    )
    carried = entry_state + earlier_sum(local_state)

    outs = []
    for i in range(CHUNKS):
        query_feat = qf_parts[i]
        phi_query = taylor(query_feat)
        cross = jnp.einsum("thf,hfv->thv", phi_query, carried, precision=highest)
        sims = jnp.einsum(
            "thf,shf->hts", query_feat, key_feat, precision=highest
        ) / math.sqrt(FEAT)
        causal = (i * size + jnp.arange(size))[:, None] >= jnp.arange(tok_rows)[None, :]
        weights = jnp.where(causal[None], 1.0 + sims + 0.5 * sims * sims, 0.0).astype(jnp.bfloat16)
        intra = jnp.einsum("hts,shv->thv", weights, lvalues, preferred_element_type=jnp.float32)
        lin_out = cross + intra
        scale = lax.rsqrt(jnp.mean(lin_out * lin_out, axis=-1, keepdims=True) + 1e-05)
        lin_normed = (
            (lin_out * scale * out_gain[None]).astype(jnp.bfloat16).reshape(size, lin_heads * VDIM)
        )
        lin_part = head_reduce_scatter(lin_normed, wo_linear)
        outs.append((after_parts[i].astype(jnp.float32) + lin_part).astype(jnp.bfloat16))
    return jnp.concatenate(outs, axis=0)


def solution(mesh):
    in_specs = (
        P(("groups", "ctx"), "head"),
        P(),
        P(None, "head"),
        P(None, "head"),
        P(None, "head"),
        P("head", None),
        P(),
        P(None, "head"),
        P(None, "head"),
        P("head", None),
        P("head", None),
        P(("groups", "head"), None, None),
    )
    out_specs = P(("groups", "ctx"), "head")
    return jax.shard_map(body, mesh=mesh, in_specs=in_specs, out_specs=out_specs, check_vma=False)
```

```python
import math

import jax
import jax.numpy as jnp
from jax import lax
from jax.sharding import PartitionSpec as P

HEAD = 128
WINDOW = 64
FEAT = 16
VDIM = 256


def from_behind(value, axis, by):
    devices = lax.axis_size(axis)
    pairs = [(i, i + by) for i in range(devices) if 0 <= i + by < devices]
    return lax.ppermute(value, axis, pairs)


def head_layout():
    devices = lax.axis_size("head")
    return devices, devices // 2


def core_swap(value):
    devices = lax.axis_size("head")
    return lax.ppermute(value, "head", [(h, h ^ 1) for h in range(devices)])


def chip_shift(value, by):
    devices, chips = head_layout()
    pairs = [(h, ((h // 2 + by) % chips) * 2 + h % 2) for h in range(devices)]
    return lax.ppermute(value, "head", pairs)


def head_reduce_scatter(lhs, weight):
    devices, chips = head_layout()
    me = lax.axis_index("head")
    core, chip = me % 2, me // 2
    width = weight.shape[1] // devices

    def block(which, offset):
        col = (((chip + offset) % chips) * 2 + which) * width
        cols = lax.dynamic_slice_in_dim(weight, col, width, axis=1)
        return jnp.dot(lhs, cols, preferred_element_type=jnp.float32)

    order = [chips - 1 - j for j in range(chips)]
    on_chip = {}
    for offset in order:
        on_chip[offset] = block(core, offset) + core_swap(block(1 - core, offset))
    acc = on_chip[chips - 1]
    for step in range(chips - 1):
        got = chip_shift(acc.astype(jnp.bfloat16), 1).astype(jnp.float32)
        acc = got + on_chip[(chips - step - 2) % chips]
    return acc


def gather_sources():
    devices, chips = head_layout()
    me = lax.axis_index("head")
    core, chip = me % 2, me // 2
    ring = [((chip + chips - step - 1) % chips) * 2 for step in range(chips - 1)]
    return [me] + [r + core for r in ring] + [me ^ 1] + [r + 1 - core for r in ring]


def head_all_gather(piece):
    devices, chips = head_layout()
    pieces = [piece, None]
    pieces[1] = core_swap(piece)
    ring, cur = [], piece
    for step in range(chips - 1):
        cur = chip_shift(cur, 1)
        ring.append(cur)
    forwarded = [core_swap(r) for r in ring]
    return jnp.concatenate([piece] + ring + [pieces[1]] + forwarded, axis=1)


def gathered_rows(weight):
    devices, chips = head_layout()
    block = weight.shape[0] // devices
    return jnp.concatenate(
        [lax.dynamic_slice_in_dim(weight, src * block, block, axis=0) for src in gather_sources()],
        axis=0,
    )


def earlier_sum(local):
    count = lax.axis_size("ctx")
    running = local
    total = jnp.zeros(local.shape, jnp.float32)
    by = 1
    while by < count:
        pairs = [(i, i + by) for i in range(count - by)]
        got = lax.ppermute(running.astype(jnp.bfloat16), "ctx", pairs).astype(jnp.float32)
        total = total + got
        running = running + got
        by *= 2
    return total


def norm_rows(values, gain):
    wide = values.astype(jnp.float32)
    scale = lax.rsqrt(jnp.mean(wide * wide, axis=-1, keepdims=True) + 1e-05)
    return (wide * scale * gain).astype(jnp.bfloat16)


def taylor(inputs):
    width = inputs.shape[-1]
    outer = (inputs[..., :, None] * inputs[..., None, :]).reshape(
        inputs.shape[:-1] + (width * width,)
    )
    ones = jnp.ones(inputs.shape[:-1] + (1,), jnp.float32)
    return jnp.concatenate(
        [ones, inputs / width**0.25, outer / (math.sqrt(2.0) * math.sqrt(width))], axis=-1
    )


CHUNKS = 1


def body(
    hidden_in,
    attn_gain,
    w_query,
    w_keys,
    w_values,
    wo_attn,
    lin_gain,
    w_feature,
    wv_linear,
    out_gain,
    wo_linear,
    entry_state,
):
    tok_rows = hidden_in.shape[0]
    size = tok_rows // CHUNKS
    kv_cols = w_keys.shape[1]
    kv_heads = kv_cols // HEAD
    group = w_query.shape[1] // HEAD // kv_heads
    hidden_parts = [hidden_in[i * size : (i + 1) * size] for i in range(CHUNKS)]
    attn_gain = gathered_rows(attn_gain)
    w_query = gathered_rows(w_query)
    w_keys = gathered_rows(w_keys)
    w_values = gathered_rows(w_values)
    lin_gain = gathered_rows(lin_gain)
    w_feature = gathered_rows(w_feature)
    wv_linear = gathered_rows(wv_linear)

    query_parts, kv_parts = [], []
    for part in hidden_parts:
        normed = norm_rows(head_all_gather(part), attn_gain)
        query_parts.append(
            jnp.dot(normed, w_query, preferred_element_type=jnp.float32).astype(jnp.bfloat16)
        )
        keys = jnp.dot(normed, w_keys, preferred_element_type=jnp.float32).astype(jnp.bfloat16)
        values = jnp.dot(normed, w_values, preferred_element_type=jnp.float32).astype(jnp.bfloat16)
        kv_parts.append(jnp.concatenate([keys, values], axis=1))
    rim = from_behind(kv_parts[-1][size - WINDOW :], "ctx", 1)
    kv_all = jnp.concatenate([rim] + kv_parts, axis=0)
    start = lax.axis_index("ctx") * tok_rows

    after_parts, after_whole_parts = [], []
    for i in range(CHUNKS):
        kv_win = kv_all[i * size : i * size + size + WINDOW]
        key_win = kv_win[:, :kv_cols].reshape(size + WINDOW, kv_heads, HEAD)
        value_win = kv_win[:, kv_cols:].reshape(size + WINDOW, kv_heads, HEAD)
        query_heads = query_parts[i].reshape(size, kv_heads, group, HEAD)
        scores = jnp.einsum(
            "tkgd,skd->kgts", query_heads, key_win, preferred_element_type=jnp.float32
        ) / math.sqrt(HEAD)
        qpos = start + i * size + jnp.arange(size, dtype=jnp.int32)
        kpos = start + i * size - WINDOW + jnp.arange(size + WINDOW, dtype=jnp.int32)
        visible = (
            (kpos[None, :] <= qpos[:, None])
            & (kpos[None, :] > qpos[:, None] - WINDOW)
            & (kpos[None, :] >= 0)
        )
        scores = jnp.where(visible, scores, -jnp.inf)
        top = jnp.max(scores, axis=-1, keepdims=True)
        expd = jnp.exp(scores - top)
        probs = (expd / jnp.sum(expd, axis=-1, keepdims=True)).astype(jnp.bfloat16)
        attended = jnp.einsum(
            "kgts,skd->tkgd", probs, value_win, preferred_element_type=jnp.float32
        )
        attended = attended.astype(jnp.bfloat16).reshape(size, -1)
        partial_out = head_reduce_scatter(attended, wo_attn)
        after_window = (hidden_parts[i].astype(jnp.float32) + partial_out).astype(jnp.bfloat16)
        after_parts.append(after_window)
        after_whole_parts.append(head_all_gather(after_window))

    qf_parts, kf_parts, lv_parts = [], [], []
    for i in range(CHUNKS):
        normed2 = norm_rows(after_whole_parts[i], lin_gain)
        feats = jnp.dot(normed2, w_feature, preferred_element_type=jnp.float32)
        lin_heads = feats.shape[1] // (2 * FEAT)
        feats = feats.reshape(size, lin_heads, 2, FEAT)
        qf_parts.append(feats[:, :, 0, :])
        kf_parts.append(feats[:, :, 1, :])
        lv_parts.append(
            jnp.dot(normed2, wv_linear, preferred_element_type=jnp.float32)
            .astype(jnp.bfloat16)
            .reshape(size, lin_heads, VDIM)
        )
    key_feat = jnp.concatenate(kf_parts, axis=0)
    lvalues = jnp.concatenate(lv_parts, axis=0)
    lin_heads = key_feat.shape[1]
    highest = lax.Precision.HIGHEST
    phi_key = taylor(key_feat)
    local_state = jnp.einsum(
        "thf,thv->hfv", phi_key, lvalues.astype(jnp.float32), precision=highest
    )
    carried = entry_state + earlier_sum(local_state)

    outs = []
    for i in range(CHUNKS):
        query_feat = qf_parts[i]
        phi_query = taylor(query_feat)
        cross = jnp.einsum("thf,hfv->thv", phi_query, carried, precision=highest)
        sims = jnp.einsum(
            "thf,shf->hts", query_feat, key_feat, precision=highest
        ) / math.sqrt(FEAT)
        causal = (i * size + jnp.arange(size))[:, None] >= jnp.arange(tok_rows)[None, :]
        weights = jnp.where(causal[None], 1.0 + sims + 0.5 * sims * sims, 0.0).astype(jnp.bfloat16)
        intra = jnp.einsum("hts,shv->thv", weights, lvalues, preferred_element_type=jnp.float32)
        lin_out = cross + intra
        scale = lax.rsqrt(jnp.mean(lin_out * lin_out, axis=-1, keepdims=True) + 1e-05)
        lin_normed = (
            (lin_out * scale * out_gain[None]).astype(jnp.bfloat16).reshape(size, lin_heads * VDIM)
        )
        lin_part = head_reduce_scatter(lin_normed, wo_linear)
        outs.append((after_parts[i].astype(jnp.float32) + lin_part).astype(jnp.bfloat16))
    return jnp.concatenate(outs, axis=0)


def solution(mesh):
    in_specs = (
        P(("groups", "ctx"), "head"),
        P(),
        P(None, "head"),
        P(None, "head"),
        P(None, "head"),
        P("head", None),
        P(),
        P(None, "head"),
        P(None, "head"),
        P("head", None),
        P("head", None),
        P(("groups", "head"), None, None),
    )
    out_specs = P(("groups", "ctx"), "head")
    return jax.shard_map(body, mesh=mesh, in_specs=in_specs, out_specs=out_specs, check_vma=False)
```

```python
import math

import jax
import jax.numpy as jnp
from jax import lax
from jax.sharding import PartitionSpec as P

HEAD = 128
WINDOW = 64
FEAT = 16
VDIM = 256


def from_behind(value, axis, by):
    devices = lax.axis_size(axis)
    pairs = [(i, i + by) for i in range(devices) if 0 <= i + by < devices]
    return lax.ppermute(value, axis, pairs)


def head_layout():
    devices = lax.axis_size("head")
    return devices, devices // 2


def core_swap(value):
    devices = lax.axis_size("head")
    return lax.ppermute(value, "head", [(h, h ^ 1) for h in range(devices)])


def chip_shift(value, by):
    devices, chips = head_layout()
    pairs = [(h, ((h // 2 + by) % chips) * 2 + h % 2) for h in range(devices)]
    return lax.ppermute(value, "head", pairs)


def head_reduce_scatter(lhs, weight):
    devices, chips = head_layout()
    me = lax.axis_index("head")
    core, chip = me % 2, me // 2
    width = weight.shape[1] // devices

    def block(which, offset):
        col = (((chip + offset) % chips) * 2 + which) * width
        cols = lax.dynamic_slice_in_dim(weight, col, width, axis=1)
        return jnp.dot(lhs, cols, preferred_element_type=jnp.float32)

    order = [chips - 1 - j for j in range(chips)]
    on_chip = {}
    for offset in order:
        on_chip[offset] = block(core, offset) + core_swap(block(1 - core, offset))
    acc = on_chip[chips - 1]
    for step in range(chips - 1):
        got = chip_shift(acc.astype(jnp.bfloat16), 1).astype(jnp.float32)
        acc = got + on_chip[(chips - step - 2) % chips]
    return acc


def gather_sources():
    devices, chips = head_layout()
    me = lax.axis_index("head")
    core, chip = me % 2, me // 2
    ring = [((chip + chips - step - 1) % chips) * 2 for step in range(chips - 1)]
    return [me] + [r + core for r in ring] + [me ^ 1] + [r + 1 - core for r in ring]


def head_all_gather(piece):
    devices, chips = head_layout()
    pieces = [piece, None]
    pieces[1] = core_swap(piece)
    ring, cur = [], piece
    for step in range(chips - 1):
        cur = chip_shift(cur, 1)
        ring.append(cur)
    forwarded = [core_swap(r) for r in ring]
    return jnp.concatenate([piece] + ring + [pieces[1]] + forwarded, axis=1)


def gathered_rows(weight):
    devices, chips = head_layout()
    block = weight.shape[0] // devices
    return jnp.concatenate(
        [lax.dynamic_slice_in_dim(weight, src * block, block, axis=0) for src in gather_sources()],
        axis=0,
    )


def earlier_sum(local):
    count = lax.axis_size("ctx")
    running = local
    total = jnp.zeros(local.shape, jnp.float32)
    by = 1
    while by < count:
        pairs = [(i, i + by) for i in range(count - by)]
        got = lax.ppermute(running.astype(jnp.bfloat16), "ctx", pairs).astype(jnp.float32)
        total = total + got
        running = running + got
        by *= 2
    return total


def norm_rows(values, gain):
    wide = values.astype(jnp.float32)
    scale = lax.rsqrt(jnp.mean(wide * wide, axis=-1, keepdims=True) + 1e-05)
    return (wide * scale * gain).astype(jnp.bfloat16)


def taylor(inputs):
    width = inputs.shape[-1]
    outer = (inputs[..., :, None] * inputs[..., None, :]).reshape(
        inputs.shape[:-1] + (width * width,)
    )
    ones = jnp.ones(inputs.shape[:-1] + (1,), jnp.float32)
    return jnp.concatenate(
        [ones, inputs / width**0.25, outer / (math.sqrt(2.0) * math.sqrt(width))], axis=-1
    )


CHUNKS = 1


def body(
    hidden_in,
    attn_gain,
    w_query,
    w_keys,
    w_values,
    wo_attn,
    lin_gain,
    w_feature,
    wv_linear,
    out_gain,
    wo_linear,
    entry_state,
):
    tok_rows = hidden_in.shape[0]
    size = tok_rows // CHUNKS
    kv_cols = w_keys.shape[1]
    kv_heads = kv_cols // HEAD
    group = w_query.shape[1] // HEAD // kv_heads
    hidden_parts = [hidden_in[i * size : (i + 1) * size] for i in range(CHUNKS)]
    attn_gain = gathered_rows(attn_gain)
    w_query = gathered_rows(w_query)
    w_keys = gathered_rows(w_keys)
    w_values = gathered_rows(w_values)
    lin_gain = gathered_rows(lin_gain)
    w_feature = gathered_rows(w_feature)
    wv_linear = gathered_rows(wv_linear)

    query_parts, kv_parts = [], []
    for part in hidden_parts:
        normed = norm_rows(head_all_gather(part), attn_gain)
        query_parts.append(
            jnp.dot(normed, w_query, preferred_element_type=jnp.float32).astype(jnp.bfloat16)
        )
        keys = jnp.dot(normed, w_keys, preferred_element_type=jnp.float32).astype(jnp.bfloat16)
        values = jnp.dot(normed, w_values, preferred_element_type=jnp.float32).astype(jnp.bfloat16)
        kv_parts.append(jnp.concatenate([keys, values], axis=1))
    rim = from_behind(kv_parts[-1][size - WINDOW :], "ctx", 1)
    kv_all = jnp.concatenate([rim] + kv_parts, axis=0)
    start = lax.axis_index("ctx") * tok_rows

    after_parts, after_whole_parts = [], []
    for i in range(CHUNKS):
        kv_win = kv_all[i * size : i * size + size + WINDOW]
        key_win = kv_win[:, :kv_cols].reshape(size + WINDOW, kv_heads, HEAD)
        value_win = kv_win[:, kv_cols:].reshape(size + WINDOW, kv_heads, HEAD)
        query_heads = query_parts[i].reshape(size, kv_heads, group, HEAD)
        scores = jnp.einsum(
            "tkgd,skd->kgts", query_heads, key_win, preferred_element_type=jnp.float32
        ) / math.sqrt(HEAD)
        qpos = start + i * size + jnp.arange(size, dtype=jnp.int32)
        kpos = start + i * size - WINDOW + jnp.arange(size + WINDOW, dtype=jnp.int32)
        visible = (
            (kpos[None, :] <= qpos[:, None])
            & (kpos[None, :] > qpos[:, None] - WINDOW)
            & (kpos[None, :] >= 0)
        )
        scores = jnp.where(visible, scores, -jnp.inf)
        top = jnp.max(scores, axis=-1, keepdims=True)
        expd = jnp.exp(scores - top)
        probs = (expd / jnp.sum(expd, axis=-1, keepdims=True)).astype(jnp.bfloat16)
        attended = jnp.einsum(
            "kgts,skd->tkgd", probs, value_win, preferred_element_type=jnp.float32
        )
        attended = attended.astype(jnp.bfloat16).reshape(size, -1)
        partial_out = head_reduce_scatter(attended, wo_attn)
        after_window = (hidden_parts[i].astype(jnp.float32) + partial_out).astype(jnp.bfloat16)
        after_parts.append(after_window)
        after_whole_parts.append(head_all_gather(after_window))

    qf_parts, kf_parts, lv_parts = [], [], []
    for i in range(CHUNKS):
        normed2 = norm_rows(after_whole_parts[i], lin_gain)
        feats = jnp.dot(normed2, w_feature, preferred_element_type=jnp.float32)
        lin_heads = feats.shape[1] // (2 * FEAT)
        feats = feats.reshape(size, lin_heads, 2, FEAT)
        qf_parts.append(feats[:, :, 0, :])
        kf_parts.append(feats[:, :, 1, :])
        lv_parts.append(
            jnp.dot(normed2, wv_linear, preferred_element_type=jnp.float32)
            .astype(jnp.bfloat16)
            .reshape(size, lin_heads, VDIM)
        )
    key_feat = jnp.concatenate(kf_parts, axis=0)
    lvalues = jnp.concatenate(lv_parts, axis=0)
    lin_heads = key_feat.shape[1]
    highest = lax.Precision.HIGHEST
    phi_key = taylor(key_feat)
    local_state = jnp.einsum(
        "thf,thv->hfv", phi_key, lvalues.astype(jnp.float32), precision=highest
    )
    prior = earlier_sum(local_state)

    outs = []
    for i in range(CHUNKS):
        query_feat = qf_parts[i]
        phi_query = taylor(query_feat)
        own = jnp.einsum("thf,hfv->thv", phi_query, entry_state, precision=highest)
        sims = jnp.einsum(
            "thf,shf->hts", query_feat, key_feat, precision=highest
        ) / math.sqrt(FEAT)
        causal = (i * size + jnp.arange(size))[:, None] >= jnp.arange(tok_rows)[None, :]
        weights = jnp.where(causal[None], 1.0 + sims + 0.5 * sims * sims, 0.0).astype(jnp.bfloat16)
        intra = jnp.einsum("hts,shv->thv", weights, lvalues, preferred_element_type=jnp.float32)
        lin_out = (own + intra) + jnp.einsum("thf,hfv->thv", phi_query, prior, precision=highest)
        scale = lax.rsqrt(jnp.mean(lin_out * lin_out, axis=-1, keepdims=True) + 1e-05)
        lin_normed = (
            (lin_out * scale * out_gain[None]).astype(jnp.bfloat16).reshape(size, lin_heads * VDIM)
        )
        lin_part = head_reduce_scatter(lin_normed, wo_linear)
        outs.append((after_parts[i].astype(jnp.float32) + lin_part).astype(jnp.bfloat16))
    return jnp.concatenate(outs, axis=0)


def solution(mesh):
    in_specs = (
        P(("groups", "ctx"), "head"),
        P(),
        P(None, "head"),
        P(None, "head"),
        P(None, "head"),
        P("head", None),
        P(),
        P(None, "head"),
        P(None, "head"),
        P("head", None),
        P("head", None),
        P(("groups", "head"), None, None),
    )
    out_specs = P(("groups", "ctx"), "head")
    return jax.shard_map(body, mesh=mesh, in_specs=in_specs, out_specs=out_specs, check_vma=False)
```

```python
import math

import jax
import jax.numpy as jnp
from jax import lax
from jax.sharding import PartitionSpec as P

HEAD = 128
WINDOW = 64
FEAT = 16
VDIM = 256


def from_behind(value, axis, by):
    devices = lax.axis_size(axis)
    pairs = [(i, i + by) for i in range(devices) if 0 <= i + by < devices]
    return lax.ppermute(value, axis, pairs)


def head_layout():
    devices = lax.axis_size("head")
    return devices, devices // 2


def core_swap(value):
    devices = lax.axis_size("head")
    return lax.ppermute(value, "head", [(h, h ^ 1) for h in range(devices)])


def chip_shift(value, by):
    devices, chips = head_layout()
    pairs = [(h, ((h // 2 + by) % chips) * 2 + h % 2) for h in range(devices)]
    return lax.ppermute(value, "head", pairs)


def head_reduce_scatter(lhs, weight):
    devices, chips = head_layout()
    me = lax.axis_index("head")
    core, chip = me % 2, me // 2
    width = weight.shape[1] // devices

    def block(which, offset):
        col = (((chip + offset) % chips) * 2 + which) * width
        cols = lax.dynamic_slice_in_dim(weight, col, width, axis=1)
        return jnp.dot(lhs, cols, preferred_element_type=jnp.float32)

    order = [chips - 1 - j for j in range(chips)]
    on_chip = {}
    for offset in order:
        on_chip[offset] = block(core, offset) + core_swap(block(1 - core, offset))
    acc = on_chip[chips - 1]
    for step in range(chips - 1):
        got = chip_shift(acc.astype(jnp.bfloat16), 1).astype(jnp.float32)
        acc = got + on_chip[(chips - step - 2) % chips]
    return acc


def gather_sources():
    devices, chips = head_layout()
    me = lax.axis_index("head")
    core, chip = me % 2, me // 2
    ring = [((chip + chips - step - 1) % chips) * 2 for step in range(chips - 1)]
    return [me] + [r + core for r in ring] + [me ^ 1] + [r + 1 - core for r in ring]


def head_all_gather(piece, dep=None):
    devices, chips = head_layout()
    pieces = [piece, None]
    pieces[1] = core_swap(piece)
    ring, cur = [], piece
    for step in range(chips - 1):
        cur = chip_shift(cur, 1)
        ring.append(cur)
    if dep is not None:
        ring = [lax.optimization_barrier((r, dep))[0] for r in ring]
    forwarded = [core_swap(r) for r in ring]
    return jnp.concatenate([piece] + ring + [pieces[1]] + forwarded, axis=1)


def gathered_rows(weight):
    devices, chips = head_layout()
    block = weight.shape[0] // devices
    return jnp.concatenate(
        [lax.dynamic_slice_in_dim(weight, src * block, block, axis=0) for src in gather_sources()],
        axis=0,
    )


def earlier_sum(local):
    count = lax.axis_size("ctx")
    running = local
    total = jnp.zeros(local.shape, jnp.float32)
    by = 1
    while by < count:
        pairs = [(i, i + by) for i in range(count - by)]
        got = lax.ppermute(running.astype(jnp.bfloat16), "ctx", pairs).astype(jnp.float32)
        total = total + got
        running = running + got
        by *= 2
    return total


def norm_rows(values, gain):
    wide = values.astype(jnp.float32)
    scale = lax.rsqrt(jnp.mean(wide * wide, axis=-1, keepdims=True) + 1e-05)
    return (wide * scale * gain).astype(jnp.bfloat16)


def taylor(inputs):
    width = inputs.shape[-1]
    outer = (inputs[..., :, None] * inputs[..., None, :]).reshape(
        inputs.shape[:-1] + (width * width,)
    )
    ones = jnp.ones(inputs.shape[:-1] + (1,), jnp.float32)
    return jnp.concatenate(
        [ones, inputs / width**0.25, outer / (math.sqrt(2.0) * math.sqrt(width))], axis=-1
    )


CHUNKS = 1


def body(
    hidden_in,
    attn_gain,
    w_query,
    w_keys,
    w_values,
    wo_attn,
    lin_gain,
    w_feature,
    wv_linear,
    out_gain,
    wo_linear,
    entry_state,
):
    tok_rows = hidden_in.shape[0]
    size = tok_rows // CHUNKS
    kv_cols = w_keys.shape[1]
    kv_heads = kv_cols // HEAD
    group = w_query.shape[1] // HEAD // kv_heads
    hidden_parts = [hidden_in[i * size : (i + 1) * size] for i in range(CHUNKS)]
    attn_gain = gathered_rows(attn_gain)
    w_query = gathered_rows(w_query)
    w_keys = gathered_rows(w_keys)
    w_values = gathered_rows(w_values)
    lin_gain = gathered_rows(lin_gain)
    w_feature = gathered_rows(w_feature)
    wv_linear = gathered_rows(wv_linear)

    query_parts, kv_parts = [], []
    for part in hidden_parts:
        ready = (attn_gain, w_query, w_keys, w_values, lin_gain, w_feature, wv_linear)
        normed = norm_rows(head_all_gather(part, ready), attn_gain)
        query_parts.append(
            jnp.dot(normed, w_query, preferred_element_type=jnp.float32).astype(jnp.bfloat16)
        )
        keys = jnp.dot(normed, w_keys, preferred_element_type=jnp.float32).astype(jnp.bfloat16)
        values = jnp.dot(normed, w_values, preferred_element_type=jnp.float32).astype(jnp.bfloat16)
        kv_parts.append(jnp.concatenate([keys, values], axis=1))
    rim = from_behind(kv_parts[-1][size - WINDOW :], "ctx", 1)
    kv_all = jnp.concatenate([rim] + kv_parts, axis=0)
    start = lax.axis_index("ctx") * tok_rows

    after_parts, after_whole_parts = [], []
    for i in range(CHUNKS):
        kv_win = kv_all[i * size : i * size + size + WINDOW]
        key_win = kv_win[:, :kv_cols].reshape(size + WINDOW, kv_heads, HEAD)
        value_win = kv_win[:, kv_cols:].reshape(size + WINDOW, kv_heads, HEAD)
        query_heads = query_parts[i].reshape(size, kv_heads, group, HEAD)
        scores = jnp.einsum(
            "tkgd,skd->kgts", query_heads, key_win, preferred_element_type=jnp.float32
        ) / math.sqrt(HEAD)
        qpos = start + i * size + jnp.arange(size, dtype=jnp.int32)
        kpos = start + i * size - WINDOW + jnp.arange(size + WINDOW, dtype=jnp.int32)
        visible = (
            (kpos[None, :] <= qpos[:, None])
            & (kpos[None, :] > qpos[:, None] - WINDOW)
            & (kpos[None, :] >= 0)
        )
        scores = jnp.where(visible, scores, -jnp.inf)
        top = jnp.max(scores, axis=-1, keepdims=True)
        expd = jnp.exp(scores - top)
        probs = (expd / jnp.sum(expd, axis=-1, keepdims=True)).astype(jnp.bfloat16)
        attended = jnp.einsum(
            "kgts,skd->tkgd", probs, value_win, preferred_element_type=jnp.float32
        )
        attended = attended.astype(jnp.bfloat16).reshape(size, -1)
        partial_out = head_reduce_scatter(attended, wo_attn)
        after_window = (hidden_parts[i].astype(jnp.float32) + partial_out).astype(jnp.bfloat16)
        after_parts.append(after_window)
        after_whole_parts.append(head_all_gather(after_window))

    qf_parts, kf_parts, lv_parts = [], [], []
    for i in range(CHUNKS):
        normed2 = norm_rows(after_whole_parts[i], lin_gain)
        feats = jnp.dot(normed2, w_feature, preferred_element_type=jnp.float32)
        lin_heads = feats.shape[1] // (2 * FEAT)
        feats = feats.reshape(size, lin_heads, 2, FEAT)
        qf_parts.append(feats[:, :, 0, :])
        kf_parts.append(feats[:, :, 1, :])
        lv_parts.append(
            jnp.dot(normed2, wv_linear, preferred_element_type=jnp.float32)
            .astype(jnp.bfloat16)
            .reshape(size, lin_heads, VDIM)
        )
    key_feat = jnp.concatenate(kf_parts, axis=0)
    lvalues = jnp.concatenate(lv_parts, axis=0)
    lin_heads = key_feat.shape[1]
    highest = lax.Precision.HIGHEST
    phi_key = taylor(key_feat)
    local_state = jnp.einsum(
        "thf,thv->hfv", phi_key, lvalues.astype(jnp.float32), precision=highest
    )
    carried = entry_state + earlier_sum(local_state)

    outs = []
    for i in range(CHUNKS):
        query_feat = qf_parts[i]
        phi_query = taylor(query_feat)
        cross = jnp.einsum("thf,hfv->thv", phi_query, carried, precision=highest)
        sims = jnp.einsum(
            "thf,shf->hts", query_feat, key_feat, precision=highest
        ) / math.sqrt(FEAT)
        causal = (i * size + jnp.arange(size))[:, None] >= jnp.arange(tok_rows)[None, :]
        weights = jnp.where(causal[None], 1.0 + sims + 0.5 * sims * sims, 0.0).astype(jnp.bfloat16)
        intra = jnp.einsum("hts,shv->thv", weights, lvalues, preferred_element_type=jnp.float32)
        lin_out = cross + intra
        scale = lax.rsqrt(jnp.mean(lin_out * lin_out, axis=-1, keepdims=True) + 1e-05)
        lin_normed = (
            (lin_out * scale * out_gain[None]).astype(jnp.bfloat16).reshape(size, lin_heads * VDIM)
        )
        lin_part = head_reduce_scatter(lin_normed, wo_linear)
        outs.append((after_parts[i].astype(jnp.float32) + lin_part).astype(jnp.bfloat16))
    return jnp.concatenate(outs, axis=0)


def solution(mesh):
    in_specs = (
        P(("groups", "ctx"), "head"),
        P(),
        P(None, "head"),
        P(None, "head"),
        P(None, "head"),
        P("head", None),
        P(),
        P(None, "head"),
        P(None, "head"),
        P("head", None),
        P("head", None),
        P(("groups", "head"), None, None),
    )
    out_specs = P(("groups", "ctx"), "head")
    return jax.shard_map(body, mesh=mesh, in_specs=in_specs, out_specs=out_specs, check_vma=False)
```

```python
import math

import jax
import jax.numpy as jnp
from jax import lax
from jax.sharding import PartitionSpec as P

HEAD = 128
WINDOW = 64
FEAT = 16
VDIM = 256


def from_behind(value, axis, by):
    devices = lax.axis_size(axis)
    pairs = [(i, i + by) for i in range(devices) if 0 <= i + by < devices]
    return lax.ppermute(value, axis, pairs)


def head_layout():
    devices = lax.axis_size("head")
    return devices, devices // 2


def core_swap(value):
    devices = lax.axis_size("head")
    return lax.ppermute(value, "head", [(h, h ^ 1) for h in range(devices)])


def chip_shift(value, by):
    devices, chips = head_layout()
    pairs = [(h, ((h // 2 + by) % chips) * 2 + h % 2) for h in range(devices)]
    return lax.ppermute(value, "head", pairs)


def head_reduce_scatter(lhs, weight):
    devices, chips = head_layout()
    me = lax.axis_index("head")
    core, chip = me % 2, me // 2
    width = weight.shape[1] // devices

    def block(which, offset):
        col = (((chip + offset) % chips) * 2 + which) * width
        cols = lax.dynamic_slice_in_dim(weight, col, width, axis=1)
        return jnp.dot(lhs, cols, preferred_element_type=jnp.float32)

    order = [chips - 1 - j for j in range(chips)]
    on_chip = {}
    for offset in order:
        on_chip[offset] = block(core, offset) + core_swap(block(1 - core, offset))
    acc = on_chip[chips - 1]
    for step in range(chips - 1):
        got = chip_shift(acc.astype(jnp.bfloat16), 1).astype(jnp.float32)
        acc = got + on_chip[(chips - step - 2) % chips]
    return acc


def gather_sources():
    devices, chips = head_layout()
    me = lax.axis_index("head")
    core, chip = me % 2, me // 2
    ring = [((chip + chips - step - 1) % chips) * 2 for step in range(chips - 1)]
    return [me] + [r + core for r in ring] + [me ^ 1] + [r + 1 - core for r in ring]


def head_all_gather(piece, dep=None):
    devices, chips = head_layout()
    pieces = [piece, None]
    pieces[1] = core_swap(piece)
    ring, cur = [], piece
    for step in range(chips - 1):
        cur = chip_shift(cur, 1)
        ring.append(cur)
    if dep is not None:
        ring = [lax.optimization_barrier((r, dep))[0] for r in ring]
    forwarded = [core_swap(r) for r in ring]
    return jnp.concatenate([piece] + ring + [pieces[1]] + forwarded, axis=1)


def gathered_rows(weight):
    devices, chips = head_layout()
    block = weight.shape[0] // devices
    return jnp.concatenate(
        [lax.dynamic_slice_in_dim(weight, src * block, block, axis=0) for src in gather_sources()],
        axis=0,
    )


def earlier_sum(local):
    count = lax.axis_size("ctx")
    running = local
    total = jnp.zeros(local.shape, jnp.float32)
    by = 1
    while by < count:
        pairs = [(i, i + by) for i in range(count - by)]
        got = lax.ppermute(running.astype(jnp.bfloat16), "ctx", pairs).astype(jnp.float32)
        total = total + got
        running = running + got
        by *= 2
    return total


def norm_rows(values, gain):
    wide = values.astype(jnp.float32)
    scale = lax.rsqrt(jnp.mean(wide * wide, axis=-1, keepdims=True) + 1e-05)
    return (wide * scale * gain).astype(jnp.bfloat16)


def taylor(inputs):
    width = inputs.shape[-1]
    outer = (inputs[..., :, None] * inputs[..., None, :]).reshape(
        inputs.shape[:-1] + (width * width,)
    )
    ones = jnp.ones(inputs.shape[:-1] + (1,), jnp.float32)
    return jnp.concatenate(
        [ones, inputs / width**0.25, outer / (math.sqrt(2.0) * math.sqrt(width))], axis=-1
    )


CHUNKS = 1


def body(
    hidden_in,
    attn_gain,
    w_query,
    w_keys,
    w_values,
    wo_attn,
    lin_gain,
    w_feature,
    wv_linear,
    out_gain,
    wo_linear,
    entry_state,
):
    tok_rows = hidden_in.shape[0]
    size = tok_rows // CHUNKS
    kv_cols = w_keys.shape[1]
    kv_heads = kv_cols // HEAD
    group = w_query.shape[1] // HEAD // kv_heads
    hidden_parts = [hidden_in[i * size : (i + 1) * size] for i in range(CHUNKS)]
    attn_gain = gathered_rows(attn_gain)
    w_query = gathered_rows(w_query)
    w_keys = gathered_rows(w_keys)
    w_values = gathered_rows(w_values)
    lin_gain = gathered_rows(lin_gain)
    w_feature = gathered_rows(w_feature)
    wv_linear = gathered_rows(wv_linear)

    query_parts, kv_parts = [], []
    for part in hidden_parts:
        ready = (attn_gain, w_query, w_keys, w_values, lin_gain, w_feature, wv_linear)
        normed = norm_rows(head_all_gather(part, ready), attn_gain)
        last_normed = normed
        query_parts.append(
            jnp.dot(normed, w_query, preferred_element_type=jnp.float32).astype(jnp.bfloat16)
        )
        keys = jnp.dot(normed, w_keys, preferred_element_type=jnp.float32).astype(jnp.bfloat16)
        values = jnp.dot(normed, w_values, preferred_element_type=jnp.float32).astype(jnp.bfloat16)
        kv_parts.append(jnp.concatenate([keys, values], axis=1))
    tail_normed = last_normed[size - WINDOW :]
    tail_kv = jnp.concatenate(
        [
            jnp.dot(tail_normed, w_keys, preferred_element_type=jnp.float32).astype(jnp.bfloat16),
            jnp.dot(tail_normed, w_values, preferred_element_type=jnp.float32).astype(jnp.bfloat16),
        ],
        axis=1,
    )
    rim = from_behind(tail_kv, "ctx", 1)
    kv_all = jnp.concatenate([rim] + kv_parts, axis=0)
    start = lax.axis_index("ctx") * tok_rows

    after_parts, after_whole_parts = [], []
    for i in range(CHUNKS):
        kv_win = kv_all[i * size : i * size + size + WINDOW]
        key_win = kv_win[:, :kv_cols].reshape(size + WINDOW, kv_heads, HEAD)
        value_win = kv_win[:, kv_cols:].reshape(size + WINDOW, kv_heads, HEAD)
        query_heads = query_parts[i].reshape(size, kv_heads, group, HEAD)
        scores = jnp.einsum(
            "tkgd,skd->kgts", query_heads, key_win, preferred_element_type=jnp.float32
        ) / math.sqrt(HEAD)
        qpos = start + i * size + jnp.arange(size, dtype=jnp.int32)
        kpos = start + i * size - WINDOW + jnp.arange(size + WINDOW, dtype=jnp.int32)
        visible = (
            (kpos[None, :] <= qpos[:, None])
            & (kpos[None, :] > qpos[:, None] - WINDOW)
            & (kpos[None, :] >= 0)
        )
        scores = jnp.where(visible, scores, -jnp.inf)
        top = jnp.max(scores, axis=-1, keepdims=True)
        expd = jnp.exp(scores - top)
        probs = (expd / jnp.sum(expd, axis=-1, keepdims=True)).astype(jnp.bfloat16)
        attended = jnp.einsum(
            "kgts,skd->tkgd", probs, value_win, preferred_element_type=jnp.float32
        )
        attended = attended.astype(jnp.bfloat16).reshape(size, -1)
        partial_out = head_reduce_scatter(attended, wo_attn)
        after_window = (hidden_parts[i].astype(jnp.float32) + partial_out).astype(jnp.bfloat16)
        after_parts.append(after_window)
        after_whole_parts.append(head_all_gather(after_window))

    qf_parts, kf_parts, lv_parts = [], [], []
    for i in range(CHUNKS):
        normed2 = norm_rows(after_whole_parts[i], lin_gain)
        feats = jnp.dot(normed2, w_feature, preferred_element_type=jnp.float32)
        lin_heads = feats.shape[1] // (2 * FEAT)
        feats = feats.reshape(size, lin_heads, 2, FEAT)
        qf_parts.append(feats[:, :, 0, :])
        kf_parts.append(feats[:, :, 1, :])
        lv_parts.append(
            jnp.dot(normed2, wv_linear, preferred_element_type=jnp.float32)
            .astype(jnp.bfloat16)
            .reshape(size, lin_heads, VDIM)
        )
    key_feat = jnp.concatenate(kf_parts, axis=0)
    lvalues = jnp.concatenate(lv_parts, axis=0)
    lin_heads = key_feat.shape[1]
    highest = lax.Precision.HIGHEST
    phi_key = taylor(key_feat)
    local_state = jnp.einsum(
        "thf,thv->hfv", phi_key, lvalues.astype(jnp.float32), precision=highest
    )
    carried = entry_state + earlier_sum(local_state)

    outs = []
    for i in range(CHUNKS):
        query_feat = qf_parts[i]
        phi_query = taylor(query_feat)
        cross = jnp.einsum("thf,hfv->thv", phi_query, carried, precision=highest)
        sims = jnp.einsum(
            "thf,shf->hts", query_feat, key_feat, precision=highest
        ) / math.sqrt(FEAT)
        causal = (i * size + jnp.arange(size))[:, None] >= jnp.arange(tok_rows)[None, :]
        weights = jnp.where(causal[None], 1.0 + sims + 0.5 * sims * sims, 0.0).astype(jnp.bfloat16)
        intra = jnp.einsum("hts,shv->thv", weights, lvalues, preferred_element_type=jnp.float32)
        lin_out = cross + intra
        scale = lax.rsqrt(jnp.mean(lin_out * lin_out, axis=-1, keepdims=True) + 1e-05)
        lin_normed = (
            (lin_out * scale * out_gain[None]).astype(jnp.bfloat16).reshape(size, lin_heads * VDIM)
        )
        lin_part = head_reduce_scatter(lin_normed, wo_linear)
        outs.append((after_parts[i].astype(jnp.float32) + lin_part).astype(jnp.bfloat16))
    return jnp.concatenate(outs, axis=0)


def solution(mesh):
    in_specs = (
        P(("groups", "ctx"), "head"),
        P(),
        P(None, "head"),
        P(None, "head"),
        P(None, "head"),
        P("head", None),
        P(),
        P(None, "head"),
        P(None, "head"),
        P("head", None),
        P("head", None),
        P(("groups", "head"), None, None),
    )
    out_specs = P(("groups", "ctx"), "head")
    return jax.shard_map(body, mesh=mesh, in_specs=in_specs, out_specs=out_specs, check_vma=False)
```

```python
import math

import jax
import jax.numpy as jnp
from jax import lax
from jax.sharding import PartitionSpec as P

HEAD = 128
WINDOW = 64
FEAT = 16
VDIM = 256


def from_behind(value, axis, by):
    devices = lax.axis_size(axis)
    pairs = [(i, i + by) for i in range(devices) if 0 <= i + by < devices]
    return lax.ppermute(value, axis, pairs)


def head_layout():
    devices = lax.axis_size("head")
    return devices, devices // 2


def core_swap(value):
    devices = lax.axis_size("head")
    return lax.ppermute(value, "head", [(h, h ^ 1) for h in range(devices)])


def chip_shift(value, by):
    devices, chips = head_layout()
    pairs = [(h, ((h // 2 + by) % chips) * 2 + h % 2) for h in range(devices)]
    return lax.ppermute(value, "head", pairs)


def head_reduce_scatter(lhs, weight):
    devices, chips = head_layout()
    me = lax.axis_index("head")
    core, chip = me % 2, me // 2
    width = weight.shape[1] // devices

    def block(which, offset):
        col = (((chip + offset) % chips) * 2 + which) * width
        cols = lax.dynamic_slice_in_dim(weight, col, width, axis=1)
        return jnp.dot(lhs, cols, preferred_element_type=jnp.float32)

    order = [chips - 1 - j for j in range(chips)]
    on_chip = {}
    for offset in order:
        on_chip[offset] = block(core, offset) + core_swap(block(1 - core, offset))
    acc = on_chip[chips - 1]
    for step in range(chips - 1):
        got = chip_shift(acc.astype(jnp.bfloat16), 1).astype(jnp.float32)
        acc = got + on_chip[(chips - step - 2) % chips]
    return acc


def gather_sources():
    devices, chips = head_layout()
    me = lax.axis_index("head")
    core, chip = me % 2, me // 2
    ring = [((chip + chips - step - 1) % chips) * 2 for step in range(chips - 1)]
    return [me] + [r + core for r in ring] + [me ^ 1] + [r + 1 - core for r in ring]


def head_all_gather(piece, dep=None):
    devices, chips = head_layout()
    pieces = [piece, None]
    pieces[1] = core_swap(piece)
    ring, cur = [], piece
    for step in range(chips - 1):
        cur = chip_shift(cur, 1)
        ring.append(cur)
    if dep is not None:
        ring = [lax.optimization_barrier((r, dep))[0] for r in ring]
    forwarded = [core_swap(r) for r in ring]
    return jnp.concatenate([piece] + ring + [pieces[1]] + forwarded, axis=1)


def gathered_rows(weight):
    devices, chips = head_layout()
    block = weight.shape[0] // devices
    return jnp.concatenate(
        [lax.dynamic_slice_in_dim(weight, src * block, block, axis=0) for src in gather_sources()],
        axis=0,
    )


def earlier_sum(local, dep):
    count = lax.axis_size("ctx")
    running = local
    total = jnp.zeros(local.shape, jnp.float32)
    by = 1
    while by < count:
        pairs = [(i, i + by) for i in range(count - by)]
        got = lax.ppermute(running.astype(jnp.bfloat16), "ctx", pairs)
        got = lax.optimization_barrier((got, dep))[0].astype(jnp.float32)
        total = total + got
        running = running + got
        by *= 2
    return total


def norm_rows(values, gain):
    wide = values.astype(jnp.float32)
    scale = lax.rsqrt(jnp.mean(wide * wide, axis=-1, keepdims=True) + 1e-05)
    return (wide * scale * gain).astype(jnp.bfloat16)


def taylor(inputs):
    width = inputs.shape[-1]
    outer = (inputs[..., :, None] * inputs[..., None, :]).reshape(
        inputs.shape[:-1] + (width * width,)
    )
    ones = jnp.ones(inputs.shape[:-1] + (1,), jnp.float32)
    return jnp.concatenate(
        [ones, inputs / width**0.25, outer / (math.sqrt(2.0) * math.sqrt(width))], axis=-1
    )


CHUNKS = 1


def body(
    hidden_in,
    attn_gain,
    w_query,
    w_keys,
    w_values,
    wo_attn,
    lin_gain,
    w_feature,
    wv_linear,
    out_gain,
    wo_linear,
    entry_state,
):
    tok_rows = hidden_in.shape[0]
    size = tok_rows // CHUNKS
    kv_cols = w_keys.shape[1]
    kv_heads = kv_cols // HEAD
    group = w_query.shape[1] // HEAD // kv_heads
    hidden_parts = [hidden_in[i * size : (i + 1) * size] for i in range(CHUNKS)]
    attn_gain = gathered_rows(attn_gain)
    w_query = gathered_rows(w_query)
    w_keys = gathered_rows(w_keys)
    w_values = gathered_rows(w_values)
    lin_gain = gathered_rows(lin_gain)
    w_feature = gathered_rows(w_feature)
    wv_linear = gathered_rows(wv_linear)

    query_parts, kv_parts = [], []
    for part in hidden_parts:
        ready = (attn_gain, w_query, w_keys, w_values, lin_gain, w_feature, wv_linear)
        normed = norm_rows(head_all_gather(part, ready), attn_gain)
        last_normed = normed
        query_parts.append(
            jnp.dot(normed, w_query, preferred_element_type=jnp.float32).astype(jnp.bfloat16)
        )
        keys = jnp.dot(normed, w_keys, preferred_element_type=jnp.float32).astype(jnp.bfloat16)
        values = jnp.dot(normed, w_values, preferred_element_type=jnp.float32).astype(jnp.bfloat16)
        kv_parts.append(jnp.concatenate([keys, values], axis=1))
    tail_normed = last_normed[size - WINDOW :]
    tail_kv = jnp.concatenate(
        [
            jnp.dot(tail_normed, w_keys, preferred_element_type=jnp.float32).astype(jnp.bfloat16),
            jnp.dot(tail_normed, w_values, preferred_element_type=jnp.float32).astype(jnp.bfloat16),
        ],
        axis=1,
    )
    rim = from_behind(tail_kv, "ctx", 1)
    kv_all = jnp.concatenate([rim] + kv_parts, axis=0)
    start = lax.axis_index("ctx") * tok_rows

    after_parts, after_whole_parts = [], []
    for i in range(CHUNKS):
        kv_win = kv_all[i * size : i * size + size + WINDOW]
        key_win = kv_win[:, :kv_cols].reshape(size + WINDOW, kv_heads, HEAD)
        value_win = kv_win[:, kv_cols:].reshape(size + WINDOW, kv_heads, HEAD)
        query_heads = query_parts[i].reshape(size, kv_heads, group, HEAD)
        scores = jnp.einsum(
            "tkgd,skd->kgts", query_heads, key_win, preferred_element_type=jnp.float32
        ) / math.sqrt(HEAD)
        qpos = start + i * size + jnp.arange(size, dtype=jnp.int32)
        kpos = start + i * size - WINDOW + jnp.arange(size + WINDOW, dtype=jnp.int32)
        visible = (
            (kpos[None, :] <= qpos[:, None])
            & (kpos[None, :] > qpos[:, None] - WINDOW)
            & (kpos[None, :] >= 0)
        )
        scores = jnp.where(visible, scores, -jnp.inf)
        top = jnp.max(scores, axis=-1, keepdims=True)
        expd = jnp.exp(scores - top)
        probs = (expd / jnp.sum(expd, axis=-1, keepdims=True)).astype(jnp.bfloat16)
        attended = jnp.einsum(
            "kgts,skd->tkgd", probs, value_win, preferred_element_type=jnp.float32
        )
        attended = attended.astype(jnp.bfloat16).reshape(size, -1)
        partial_out = head_reduce_scatter(attended, wo_attn)
        after_window = (hidden_parts[i].astype(jnp.float32) + partial_out).astype(jnp.bfloat16)
        after_parts.append(after_window)
        after_whole_parts.append(head_all_gather(after_window))

    qf_parts, kf_parts, lv_parts = [], [], []
    for i in range(CHUNKS):
        normed2 = norm_rows(after_whole_parts[i], lin_gain)
        feats = jnp.dot(normed2, w_feature, preferred_element_type=jnp.float32)
        lin_heads = feats.shape[1] // (2 * FEAT)
        feats = feats.reshape(size, lin_heads, 2, FEAT)
        qf_parts.append(feats[:, :, 0, :])
        kf_parts.append(feats[:, :, 1, :])
        lv_parts.append(
            jnp.dot(normed2, wv_linear, preferred_element_type=jnp.float32)
            .astype(jnp.bfloat16)
            .reshape(size, lin_heads, VDIM)
        )
    key_feat = jnp.concatenate(kf_parts, axis=0)
    lvalues = jnp.concatenate(lv_parts, axis=0)
    lin_heads = key_feat.shape[1]
    highest = lax.Precision.HIGHEST
    phi_key = taylor(key_feat)
    local_state = jnp.einsum(
        "thf,thv->hfv", phi_key, lvalues.astype(jnp.float32), precision=highest
    )
    intra_parts = []
    for i in range(CHUNKS):
        sims = jnp.einsum(
            "thf,shf->hts", qf_parts[i], key_feat, precision=highest
        ) / math.sqrt(FEAT)
        causal = (i * size + jnp.arange(size))[:, None] >= jnp.arange(tok_rows)[None, :]
        weights = jnp.where(causal[None], 1.0 + sims + 0.5 * sims * sims, 0.0).astype(jnp.bfloat16)
        intra_parts.append(
            jnp.einsum("hts,shv->thv", weights, lvalues, preferred_element_type=jnp.float32)
        )
    carried = entry_state + earlier_sum(local_state, intra_parts)

    outs = []
    for i in range(CHUNKS):
        query_feat = qf_parts[i]
        phi_query = taylor(query_feat)
        cross = jnp.einsum("thf,hfv->thv", phi_query, carried, precision=highest)
        intra = intra_parts[i]
        lin_out = cross + intra
        scale = lax.rsqrt(jnp.mean(lin_out * lin_out, axis=-1, keepdims=True) + 1e-05)
        lin_normed = (
            (lin_out * scale * out_gain[None]).astype(jnp.bfloat16).reshape(size, lin_heads * VDIM)
        )
        lin_part = head_reduce_scatter(lin_normed, wo_linear)
        outs.append((after_parts[i].astype(jnp.float32) + lin_part).astype(jnp.bfloat16))
    return jnp.concatenate(outs, axis=0)


def solution(mesh):
    in_specs = (
        P(("groups", "ctx"), "head"),
        P(),
        P(None, "head"),
        P(None, "head"),
        P(None, "head"),
        P("head", None),
        P(),
        P(None, "head"),
        P(None, "head"),
        P("head", None),
        P("head", None),
        P(("groups", "head"), None, None),
    )
    out_specs = P(("groups", "ctx"), "head")
    return jax.shard_map(body, mesh=mesh, in_specs=in_specs, out_specs=out_specs, check_vma=False)
```
